512 devices in a mesh: tile: 128 (over z, y, core), freq: 4 (over x).
Axes of the slice: x: 4, y: 8, z: 8, core: 2. Of those that a mesh axis runs over, the one named last changes fastest.
Arguments:
- observed: float32 [4, 4096, 128], P('freq', 'tile'), may hold values from -6 to 6
- factor_u: float32 [2, 4, 4096, 4096], P(None, 'freq', 'tile'), may hold values from -0.03125 to 0.03125
- factor_v: float32 [2, 4, 16384, 1024], P(None, 'freq', 'tile'), may hold values from -0.125 to 0.125
- tile_ranks: int32 [4, 16, 64], P('freq'), may hold values from 16 to 64
Outputs:
- estimate: float32 [16384, 1024], P('tile', 'freq')
- residual: float32 [4, 4096, 128], P('freq', 'tile')
The draws below stay inside these ranges and needn't reach their ends.
Inputs may be any that keep to these rules, and one draw needn't show every extreme that they name: Columns r >= tile_ranks[f, i, j] of tile (i, j)'s factors are padding and do not enter the kernel.
All inputs are finite; a program needn't handle non-finite values.
Results may differ from the reference program's by a relative error of at most 0.0001.
Values sent between devices are 32-bit elements; how exact they have to be, the bound alone decides.
No kernel may reach another device: no remote copies, remote signals or barrier semaphores. Data moves between devices by JAX's collectives and lax.ppermute only.
A program may use at most 64 MiB of HBM per device.

```python
import math
import jax
import jax.numpy as jnp
from jax import lax

TW = 256
R = 64
NV = 64
NT = 64
N = 16384
M = 4096
MT = 16
F = 4
TIMES = 16


mix_common = 0.9


mix_own = math.sqrt(1.0 - mix_common * mix_common)


def mixed_normal(key, common_shape, own_shape, salt):
    shared = jax.random.normal(jax.random.fold_in(key, salt), common_shape, jnp.float32)
    own_part = jax.random.normal(jax.random.fold_in(key, salt + 1), own_shape, jnp.float32)
    return mix_common * shared + mix_own * own_part


def draw_factor_u(key, part):
    common_shape = (2, 1, M, NT * R)
    own_shape = (2, F, M, NT * R)
    values = mixed_normal(key, common_shape, own_shape, 101)
    return jnp.clip(values, -2.0, 2.0) * float(NT * R) ** (-0.5)


def draw_factor_v(key, part):
    common_shape = (2, 1, N, MT * R)
    own_shape = (2, F, N, MT * R)
    values = mixed_normal(key, common_shape, own_shape, 201)
    return jnp.clip(values, -2.0, 2.0) * float(TW) ** (-0.5)


def draw_observed(key, part):
    common_shape = (1, M, 2 * NV)
    own_shape = (F, M, 2 * NV)
    values = mixed_normal(key, common_shape, own_shape, 301)
    delay_steps = jax.random.randint(jax.random.fold_in(key, 307), (), 0, TIMES)
    turn_count = (2 * jnp.arange(F, dtype=jnp.int32) + 1) * delay_steps % TIMES
    angle_rad = turn_count.astype(jnp.float32) * (2.0 * math.pi / TIMES)
    cosine_part = jnp.cos(angle_rad)[:, None, None]
    sine_part = jnp.sin(angle_rad)[:, None, None]
    real_in = values[:, :, :NV]
    imag_in = values[:, :, NV:]
    real_out = real_in * cosine_part + imag_in * sine_part
    imag_out = imag_in * cosine_part - real_in * sine_part
    return jnp.clip(jnp.concatenate([real_out, imag_out], axis=2), -6.0, 6.0)


def plant(result, own_key, low, high):
    dims = result.shape
    place = [jax.random.randint(jax.random.fold_in(own_key, axis), (), 0, dims[axis]) for axis in range(len(dims))]
    result = result.at[tuple(place)].set(low)
    longest = dims.index(max(dims))
    place[longest] = (place[longest] + 1) % dims[longest]
    return result.at[tuple(place)].set(high)


def setup_inputs(seed: int = 0) -> dict:
    key_list = jax.random.split(jax.random.key(seed), 5)
    return {
        "observed": draw_observed(jax.random.fold_in(key_list[4], 71), 0),
        "factor_u": draw_factor_u(jax.random.fold_in(key_list[4], 71), 0),
        "factor_v": draw_factor_v(jax.random.fold_in(key_list[4], 71), 0),
        "tile_ranks": plant(jax.random.randint(key_list[3], (F, MT, NT), R // 4, R + 1), jax.random.fold_in(key_list[3], 1), R // 4, R).astype(jnp.int32),
    }


step_size = 0.25
shrink_factor = 0.5
energy_floor = 1e-06
highest = lax.Precision.HIGHEST

def contract(form, left, right):
    return jnp.einsum(form, left, right, precision=highest)

def phases(freq_index, time_index, total_times):
    turn_count = (2 * freq_index[:, None] + 1) * time_index[None, :] % total_times
    angle_rad = turn_count.astype(jnp.float32) * (2.0 * math.pi / total_times)
    weight = 1.0 / math.sqrt(total_times)
    return (jnp.cos(angle_rad) * weight, jnp.sin(angle_rad) * weight)

def shrink(update):
    threshold = shrink_factor * jnp.sqrt(jnp.mean(update * update) + energy_floor)
    return update - jnp.clip(update, -threshold, threshold)

def reference(observed, factor_u, factor_v, tile_ranks):
    cosine_table, sine_table = phases(jnp.arange(F, dtype=jnp.int32), jnp.arange(TIMES, dtype=jnp.int32), TIMES)
    levels = jnp.arange(R, dtype=jnp.int32)
    masks = (levels[None, None, None, :] < tile_ranks[:, :, :, None]).astype(jnp.float32)

    def factors(freq_pos):
        u_real = factor_u[0, freq_pos].reshape(MT, TW, NT, R)
        u_imag = factor_u[1, freq_pos].reshape(MT, TW, NT, R)
        v_real = factor_v[0, freq_pos].reshape(NT, TW, MT, R)
        v_imag = factor_v[1, freq_pos].reshape(NT, TW, MT, R)
        return (u_real, u_imag, v_real, v_imag)

    def forward(series):
        results = []
        for freq_pos in range(F):
            u_real, u_imag, v_real, v_imag = factors(freq_pos)
            rank_mask = masks[freq_pos][:, :, :, None]
            x_real = contract('t,ntv->nv', cosine_table[freq_pos], series).reshape(NT, TW, NV)
            x_imag = -contract('t,ntv->nv', sine_table[freq_pos], series).reshape(NT, TW, NV)
            c_real = (contract('jnir,jnv->ijrv', v_real, x_real) + contract('jnir,jnv->ijrv', v_imag, x_imag)) * rank_mask
            c_imag = (contract('jnir,jnv->ijrv', v_real, x_imag) - contract('jnir,jnv->ijrv', v_imag, x_real)) * rank_mask
            y_real = contract('iajr,ijrv->iav', u_real, c_real) - contract('iajr,ijrv->iav', u_imag, c_imag)
            y_imag = contract('iajr,ijrv->iav', u_real, c_imag) + contract('iajr,ijrv->iav', u_imag, c_real)
            results.append(jnp.concatenate([y_real.reshape(M, NV), y_imag.reshape(M, NV)], axis=1))
        return jnp.stack(results)

    def adjoint(residual):
        gradient = jnp.zeros((N, TIMES, NV), jnp.float32)
        for freq_pos in range(F):
            u_real, u_imag, v_real, v_imag = factors(freq_pos)
            rank_mask = masks[freq_pos][:, :, :, None]
            r_real = residual[freq_pos, :, :NV].reshape(MT, TW, NV)
            r_imag = residual[freq_pos, :, NV:].reshape(MT, TW, NV)
            e_real = (contract('iajr,iav->ijrv', u_real, r_real) + contract('iajr,iav->ijrv', u_imag, r_imag)) * rank_mask
            e_imag = (contract('iajr,iav->ijrv', u_real, r_imag) - contract('iajr,iav->ijrv', u_imag, r_real)) * rank_mask
            g_real = (contract('jnir,ijrv->jnv', v_real, e_real) - contract('jnir,ijrv->jnv', v_imag, e_imag)).reshape(N, NV)
            g_imag = (contract('jnir,ijrv->jnv', v_real, e_imag) + contract('jnir,ijrv->jnv', v_imag, e_real)).reshape(N, NV)
            gradient = gradient + cosine_table[freq_pos][None, :, None] * g_real[:, None, :] - sine_table[freq_pos][None, :, None] * g_imag[:, None, :]
        return gradient
    first = shrink(-step_size * adjoint(-observed))
    residual = forward(first) - observed
    estimate = shrink(first - step_size * adjoint(residual))
    return (estimate.reshape(N, TIMES * NV), residual)
```

```python
import math

import jax
import jax.numpy as jnp
from jax import lax
from jax.sharding import PartitionSpec as P

R = 64
TIMES = 16

step_size = 0.25
shrink_factor = 0.5
energy_floor = 1e-06
highest = lax.Precision.HIGHEST


def contract(form, left, right):
    return jnp.einsum(form, left, right, precision=highest)


def phases(freq_index, time_index, total_times):
    turn_count = (2 * freq_index[:, None] + 1) * time_index[None, :] % total_times
    angle_rad = turn_count.astype(jnp.float32) * (2.0 * math.pi / total_times)
    weight = 1.0 / math.sqrt(total_times)
    return (jnp.cos(angle_rad) * weight, jnp.sin(angle_rad) * weight)


def local(observed, factor_u, factor_v, tile_ranks):
    tile_count = lax.axis_size("tile")
    freq_count = lax.axis_size("freq")
    position = lax.axis_index("tile")
    freq_pos = lax.axis_index("freq")
    core = position % 2
    column = position // 2
    rows_u = factor_u.shape[2]
    rows_v = factor_v.shape[2]
    row_tiles = factor_v.shape[3] // R
    col_tiles = factor_u.shape[3] // R
    sources = observed.shape[2] // 2
    half = sources // 2
    quarter = half // 2
    chips_per_row_tile = tile_count // row_tiles // 2
    times_here = TIMES // freq_count
    total_times = times_here * freq_count
    entries = rows_v * tile_count * total_times * sources

    pair = [(k, k ^ 1) for k in range(tile_count)]

    def swap(x):
        return lax.ppermute(x, "tile", pair)

    u_own = factor_u[:, 0]
    v_own = factor_v[:, 0]
    obs_own = observed[0]
    u_both = jnp.concatenate([u_own, swap(u_own)], axis=1)
    v_both = jnp.concatenate([v_own, swap(v_own)], axis=1)
    obs_both = jnp.concatenate([obs_own, swap(obs_own)], axis=0)
    obs_split = obs_both.reshape(2 * rows_u, 2, 2, half)
    target = lax.dynamic_index_in_dim(obs_split, core, axis=2, keepdims=False).transpose(1, 0, 2)

    rank_column = lax.dynamic_index_in_dim(tile_ranks[0], column, axis=1, keepdims=False)
    rank_mask = (jnp.arange(R, dtype=jnp.int32)[None, :] < rank_column[:, None]).astype(jnp.float32)

    all_freqs = jnp.arange(freq_count, dtype=jnp.int32)
    all_times = jnp.arange(total_times, dtype=jnp.int32)
    cos_tab, sin_tab = phases(all_freqs, all_times, total_times)

    def adjoint(resid):
        products = contract("cmk,dmv->cdkv", u_both, resid)
        e_re = products[0, 0] + products[1, 1]
        e_im = products[0, 1] - products[1, 0]
        e = jnp.stack([e_re, e_im]).reshape(2, col_tiles, R, 2, quarter)
        outgoing = e.transpose(1, 3, 0, 2, 4).reshape(tile_count, 2, R, quarter)
        incoming = lax.all_to_all(outgoing, "tile", 0, 0, tiled=True)
        gathered = incoming.reshape(row_tiles, chips_per_row_tile, 2, 2, R, quarter).sum(axis=1)
        gathered = gathered * rank_mask[:, None, None, :, None]
        coeffs = gathered.transpose(2, 0, 3, 1, 4).reshape(2, row_tiles * R, half)
        blocks = contract("cnk,dkv->cdnv", v_both, coeffs)
        g_re = blocks[0, 0] - blocks[1, 1]
        g_im = blocks[0, 1] + blocks[1, 0]
        return jnp.stack([g_re, g_im])

    def all_freq(spectrum):
        outgoing = jnp.broadcast_to(spectrum[None], (freq_count,) + spectrum.shape)
        return lax.all_to_all(outgoing, "freq", 0, 0, tiled=True)

    def to_time(spectra):
        return contract("ft,fnv->ntv", cos_tab, spectra[:, 0]) - contract(
            "ft,fnv->ntv", sin_tab, spectra[:, 1]
        )

    def shrink(update):
        energy = jnp.sum(update * update)
        outgoing = jnp.broadcast_to(energy, (tile_count, 1))
        total = jnp.sum(lax.all_to_all(outgoing, "tile", 0, 0, tiled=True))
        threshold = shrink_factor * jnp.sqrt(total / entries + energy_floor)
        return threshold

    grad1 = adjoint(target)
    update1 = step_size * to_time(all_freq(grad1))
    threshold1 = shrink(update1)
    first = update1 - jnp.clip(update1, -threshold1, threshold1)

    cos_q = lax.dynamic_index_in_dim(cos_tab, freq_pos, axis=0, keepdims=False)
    sin_q = lax.dynamic_index_in_dim(sin_tab, freq_pos, axis=0, keepdims=False)
    x_re = contract("t,ntv->nv", cos_q, first)
    x_im = -contract("t,ntv->nv", sin_q, first)
    products = contract("cnk,dnv->cdkv", v_both, jnp.stack([x_re, x_im]))
    c_re = products[0, 0] + products[1, 1]
    c_im = products[0, 1] - products[1, 0]
    coeffs = jnp.stack([c_re, c_im]).reshape(2, row_tiles, R, 2, quarter)
    coeffs = coeffs * rank_mask[None, :, :, None, None]
    outgoing = jnp.broadcast_to(
        coeffs.transpose(1, 3, 0, 2, 4)[:, None],
        (row_tiles, chips_per_row_tile, 2, 2, R, quarter),
    ).reshape(tile_count, 2, R, quarter)
    incoming = lax.all_to_all(outgoing, "tile", 0, 0, tiled=True)
    summed = incoming.reshape(col_tiles, 2, 2, R, quarter).transpose(2, 0, 3, 1, 4)
    summed = summed.reshape(2, col_tiles * R, half)
    blocks = contract("cmk,dkv->cdmv", u_both, summed)
    y_re = blocks[0, 0] - blocks[1, 1]
    y_im = blocks[0, 1] + blocks[1, 0]
    residual = jnp.stack([y_re, y_im]) - target

    grad2 = adjoint(residual)
    update2 = first - step_size * to_time(all_freq(grad2))
    threshold2 = shrink(update2)
    mine = lax.dynamic_slice_in_dim(update2, freq_pos * times_here, times_here, axis=1)
    mine = mine - jnp.clip(mine, -threshold2, threshold2)
    mine = mine.reshape(2, rows_v, times_here, 2, quarter)
    other = swap(mine[1])
    own = mine[0]
    first_b = jnp.where(core == 0, own, other)
    second_b = jnp.where(core == 0, other, own)
    estimate = jnp.stack([first_b, second_b], axis=3).reshape(rows_v, times_here * sources)

    res_other = swap(residual[:, rows_u:])
    res_own = residual[:, :rows_u]
    lo = jnp.where(core == 0, res_own, res_other)
    hi = jnp.where(core == 0, res_other, res_own)
    residual_out = jnp.stack([lo, hi], axis=2).transpose(1, 0, 2, 3).reshape(1, rows_u, 2 * sources)
    return (estimate, residual_out)


def solution(mesh):
    placed = (
        P("freq", "tile", None),
        P(None, "freq", "tile", None),
        P(None, "freq", "tile", None),
        P("freq", None, None),
    )
    return jax.shard_map(
        local,
        mesh=mesh,
        in_specs=placed,
        out_specs=(P("tile", "freq"), P("freq", "tile", None)),
        check_vma=False,
    )
```

```python
import math

import jax
import jax.numpy as jnp
from jax import lax
from jax.sharding import PartitionSpec as P

R = 64
TIMES = 16
LANES = 128

step_size = 0.25
shrink_factor = 0.5
energy_floor = 1e-06
highest = lax.Precision.HIGHEST


def contract(form, left, right):
    return jnp.einsum(form, left, right, precision=highest)


def phases(freq_index, time_index, total_times):
    turn_count = (2 * freq_index[:, None] + 1) * time_index[None, :] % total_times
    angle_rad = turn_count.astype(jnp.float32) * (2.0 * math.pi / total_times)
    weight = 1.0 / math.sqrt(total_times)
    return (jnp.cos(angle_rad) * weight, jnp.sin(angle_rad) * weight)


def local(observed, factor_u, factor_v, tile_ranks):
    tile_count = lax.axis_size("tile")
    freq_count = lax.axis_size("freq")
    position = lax.axis_index("tile")
    freq_pos = lax.axis_index("freq")
    core = position % 2
    column = position // 2
    rows_u = factor_u.shape[2]
    rows_v = factor_v.shape[2]
    row_tiles = factor_v.shape[3] // R
    col_tiles = factor_u.shape[3] // R
    sources = observed.shape[2] // 2
    half = sources // 2
    quarter = half // 2
    chips_per_row_tile = tile_count // row_tiles // 2
    times_here = TIMES // freq_count
    total_times = times_here * freq_count
    entries = rows_v * tile_count * total_times * sources
    chunk = (2 * quarter * R // LANES, LANES)

    pair = [(k, k ^ 1) for k in range(tile_count)]

    def swap(x):
        return lax.ppermute(x, "tile", pair)

    u_own = factor_u[:, 0]
    v_own = factor_v[:, 0]
    obs_own = observed[0]
    u_both = jnp.concatenate([u_own, swap(u_own)], axis=1)
    v_both = jnp.concatenate([v_own, swap(v_own)], axis=1)
    obs_both = jnp.concatenate([obs_own, swap(obs_own)], axis=0)
    obs_split = obs_both.reshape(2 * rows_u, 2, 2, half)
    target = lax.dynamic_index_in_dim(obs_split, core, axis=2, keepdims=False).transpose(1, 2, 0)

    rank_column = lax.dynamic_index_in_dim(tile_ranks[0], column, axis=1, keepdims=False)
    rank_mask = (jnp.arange(R, dtype=jnp.int32)[None, :] < rank_column[:, None]).astype(jnp.float32)

    all_freqs = jnp.arange(freq_count, dtype=jnp.int32)
    all_times = jnp.arange(total_times, dtype=jnp.int32)
    cos_tab, sin_tab = phases(all_freqs, all_times, total_times)

    def adjoint(resid):
        products = contract("dvm,cmk->dcvk", resid, u_both)
        e_re = products[0, 0] + products[1, 1]
        e_im = products[1, 0] - products[0, 1]
        e = jnp.stack([e_re, e_im]).reshape(2, 2, quarter, col_tiles, R)
        outgoing = e.transpose(3, 1, 0, 2, 4).reshape((tile_count,) + chunk)
        incoming = lax.all_to_all(outgoing, "tile", 0, 0, tiled=True)
        gathered = incoming.reshape((row_tiles, chips_per_row_tile, 2) + chunk).sum(axis=1)
        gathered = gathered.reshape(row_tiles, 2, 2, quarter, R) * rank_mask[:, None, None, None, :]
        coeffs = gathered.transpose(2, 1, 3, 0, 4).reshape(2, half, row_tiles * R)
        blocks = contract("dvk,cnk->dcvn", coeffs, v_both)
        g_re = blocks[0, 0] - blocks[1, 1]
        g_im = blocks[1, 0] + blocks[0, 1]
        return jnp.stack([g_re, g_im])

    def all_freq(spectrum):
        outgoing = jnp.broadcast_to(spectrum[None], (freq_count,) + spectrum.shape)
        return lax.all_to_all(outgoing, "freq", 0, 0, tiled=True)

    def to_time(spectra):
        total = 0.0
        for f in range(freq_count):
            total = total + (
                cos_tab[f][:, None, None] * spectra[f, 0][None]
                - sin_tab[f][:, None, None] * spectra[f, 1][None]
            )
        return total

    def threshold_of(update):
        energy = jnp.sum(update * update)
        outgoing = jnp.broadcast_to(energy, (tile_count, 1))
        total = jnp.sum(lax.all_to_all(outgoing, "tile", 0, 0, tiled=True))
        return shrink_factor * jnp.sqrt(total / entries + energy_floor)

    grad1 = adjoint(target)
    update1 = step_size * to_time(all_freq(grad1))
    threshold1 = threshold_of(update1)
    first = update1 - jnp.clip(update1, -threshold1, threshold1)

    cos_q = lax.dynamic_index_in_dim(cos_tab, freq_pos, axis=0, keepdims=False)
    sin_q = lax.dynamic_index_in_dim(sin_tab, freq_pos, axis=0, keepdims=False)
    x_re = jnp.sum(cos_q[:, None, None] * first, axis=0)
    x_im = -jnp.sum(sin_q[:, None, None] * first, axis=0)
    products = contract("dvn,cnk->dcvk", jnp.stack([x_re, x_im]), v_both)
    c_re = products[0, 0] + products[1, 1]
    c_im = products[1, 0] - products[0, 1]
    coeffs = jnp.stack([c_re, c_im]).reshape(2, 2, quarter, row_tiles, R)
    coeffs = coeffs * rank_mask[None, None, None, :, :]
    outgoing = jnp.broadcast_to(
        coeffs.transpose(3, 1, 0, 2, 4)[:, None],
        (row_tiles, chips_per_row_tile, 2, 2, quarter, R),
    ).reshape((tile_count,) + chunk)
    incoming = lax.all_to_all(outgoing, "tile", 0, 0, tiled=True)
    summed = incoming.reshape(col_tiles, 2, 2, quarter, R).transpose(2, 1, 3, 0, 4)
    summed = summed.reshape(2, half, col_tiles * R)
    blocks = contract("dvk,cmk->dcvm", summed, u_both)
    y_re = blocks[0, 0] - blocks[1, 1]
    y_im = blocks[1, 0] + blocks[0, 1]
    residual = jnp.stack([y_re, y_im]) - target

    grad2 = adjoint(residual)
    update2 = first - step_size * to_time(all_freq(grad2))
    threshold2 = threshold_of(update2)
    mine = lax.dynamic_slice_in_dim(update2, freq_pos * times_here, times_here, axis=0)
    mine = mine - jnp.clip(mine, -threshold2, threshold2)
    mine = mine.reshape(times_here, 2, quarter, 2, rows_v)
    own = mine[:, :, :, 0]
    other = swap(mine[:, :, :, 1])
    first_b = jnp.where(core == 0, own, other)
    second_b = jnp.where(core == 0, other, own)
    estimate = jnp.stack([first_b, second_b], axis=2).transpose(4, 0, 1, 2, 3)
    estimate = estimate.reshape(rows_v, times_here * sources)

    res_own = residual[:, :, :rows_u]
    res_other = swap(residual[:, :, rows_u:])
    lo = jnp.where(core == 0, res_own, res_other)
    hi = jnp.where(core == 0, res_other, res_own)
    residual_out = jnp.stack([lo, hi], axis=1).transpose(3, 0, 1, 2).reshape(1, rows_u, 2 * sources)
    return (estimate, residual_out)


def solution(mesh):
    placed = (
        P("freq", "tile", None),
        P(None, "freq", "tile", None),
        P(None, "freq", "tile", None),
        P("freq", None, None),
    )
    return jax.shard_map(
        local,
        mesh=mesh,
        in_specs=placed,
        out_specs=(P("tile", "freq"), P("freq", "tile", None)),
        check_vma=False,
    )
```

```python
import math

import jax
import jax.numpy as jnp
from jax import lax
from jax.sharding import PartitionSpec as P

R = 64
TIMES = 16
LANES = 128

step_size = 0.25
shrink_factor = 0.5
energy_floor = 1e-06
highest = lax.Precision.HIGHEST


def contract(form, left, right):
    return jnp.einsum(form, left, right, precision=highest)


def phases(freq_index, time_index, total_times):
    turn_count = (2 * freq_index[:, None] + 1) * time_index[None, :] % total_times
    angle_rad = turn_count.astype(jnp.float32) * (2.0 * math.pi / total_times)
    weight = 1.0 / math.sqrt(total_times)
    return (jnp.cos(angle_rad) * weight, jnp.sin(angle_rad) * weight)


def local(observed, factor_u, factor_v, tile_ranks):
    tile_count = lax.axis_size("tile")
    freq_count = lax.axis_size("freq")
    position = lax.axis_index("tile")
    freq_pos = lax.axis_index("freq")
    core = position % 2
    column = position // 2
    rows_u = factor_u.shape[2]
    rows_v = factor_v.shape[2]
    row_tiles = factor_v.shape[3] // R
    col_tiles = factor_u.shape[3] // R
    sources = observed.shape[2] // 2
    half = sources // 2
    quarter = half // 2
    chips_per_row_tile = tile_count // row_tiles // 2
    times_here = TIMES // freq_count
    total_times = times_here * freq_count
    entries = rows_v * tile_count * total_times * sources
    chunk = (2 * quarter * R // LANES, LANES)

    pair = [(k, k ^ 1) for k in range(tile_count)]

    def swap(x):
        return lax.ppermute(x, "tile", pair)

    u_own = factor_u[:, 0]
    v_own = factor_v[:, 0]
    obs_own = observed[0]
    u_both = jnp.concatenate([u_own, swap(u_own)], axis=1)
    v_both = jnp.concatenate([v_own, swap(v_own)], axis=1)
    obs_both = jnp.concatenate([obs_own, swap(obs_own)], axis=0)
    u_flat = u_both.reshape(2 * 2 * rows_u, col_tiles * R)
    u_rows = u_both.transpose(1, 0, 2).reshape(2 * rows_u, 2 * col_tiles * R)
    v_flat = v_both.reshape(2 * 2 * rows_v, row_tiles * R)
    v_rows = v_both.transpose(1, 0, 2).reshape(2 * rows_v, 2 * row_tiles * R)
    obs_split = obs_both.reshape(2 * rows_u, 2, 2, half)
    target = lax.dynamic_index_in_dim(obs_split, core, axis=2, keepdims=False).transpose(1, 2, 0)

    rank_column = lax.dynamic_index_in_dim(tile_ranks[0], column, axis=1, keepdims=False)
    rank_mask = (jnp.arange(R, dtype=jnp.int32)[None, :] < rank_column[:, None]).astype(jnp.float32)

    all_freqs = jnp.arange(freq_count, dtype=jnp.int32)
    all_times = jnp.arange(total_times, dtype=jnp.int32)
    cos_tab, sin_tab = phases(all_freqs, all_times, total_times)

    def adjoint(resid):
        lhs = jnp.stack([
            jnp.concatenate([resid[0], resid[1]], axis=1),
            jnp.concatenate([resid[1], -resid[0]], axis=1),
        ])
        e = contract("xvq,qk->xvk", lhs, u_flat).reshape(2, 2, quarter, col_tiles, R)
        outgoing = e.transpose(3, 1, 0, 2, 4).reshape((tile_count,) + chunk)
        incoming = lax.all_to_all(outgoing, "tile", 0, 0, tiled=True)
        gathered = incoming.reshape((row_tiles, chips_per_row_tile, 2) + chunk).sum(axis=1)
        gathered = gathered.reshape(row_tiles, 2, 2, quarter, R) * rank_mask[:, None, None, None, :]
        coeffs = gathered.transpose(2, 1, 3, 0, 4).reshape(2, half, row_tiles * R)
        lhs = jnp.stack([
            jnp.concatenate([coeffs[0], -coeffs[1]], axis=1),
            jnp.concatenate([coeffs[1], coeffs[0]], axis=1),
        ])
        return contract("xvq,nq->xvn", lhs, v_rows)

    def all_freq(spectrum):
        pieces = [spectrum] + [
            lax.ppermute(spectrum, "freq", [(f, (f + shift) % freq_count) for f in range(freq_count)])
            for shift in range(1, freq_count)
        ]
        order = (freq_pos - all_freqs) % freq_count
        return jnp.take(jnp.stack(pieces), order, axis=0)

    def to_time(spectra):
        total = 0.0
        for f in range(freq_count):
            total = total + (
                cos_tab[f][:, None, None] * spectra[f, 0][None]
                - sin_tab[f][:, None, None] * spectra[f, 1][None]
            )
        return total

    def threshold_of(update):
        energy = jnp.sum(update * update)
        outgoing = jnp.broadcast_to(energy, (tile_count, 1))
        total = jnp.sum(lax.all_to_all(outgoing, "tile", 0, 0, tiled=True))
        return shrink_factor * jnp.sqrt(total / entries + energy_floor)

    grad1 = adjoint(target)
    update1 = step_size * to_time(all_freq(grad1))
    threshold1 = threshold_of(update1)
    first = update1 - jnp.clip(update1, -threshold1, threshold1)

    cos_q = lax.dynamic_index_in_dim(cos_tab, freq_pos, axis=0, keepdims=False)
    sin_q = lax.dynamic_index_in_dim(sin_tab, freq_pos, axis=0, keepdims=False)
    x_re = jnp.sum(cos_q[:, None, None] * first, axis=0)
    x_im = -jnp.sum(sin_q[:, None, None] * first, axis=0)
    lhs = jnp.stack([
        jnp.concatenate([x_re, x_im], axis=1),
        jnp.concatenate([x_im, -x_re], axis=1),
    ])
    products = contract("xvq,qk->xvk", lhs, v_flat)
    coeffs = products.reshape(2, 2, quarter, row_tiles, R)
    coeffs = coeffs * rank_mask[None, None, None, :, :]
    outgoing = jnp.broadcast_to(
        coeffs.transpose(3, 1, 0, 2, 4)[:, None],
        (row_tiles, chips_per_row_tile, 2, 2, quarter, R),
    ).reshape((tile_count,) + chunk)
    incoming = lax.all_to_all(outgoing, "tile", 0, 0, tiled=True)
    summed = incoming.reshape(col_tiles, 2, 2, quarter, R).transpose(2, 1, 3, 0, 4)
    summed = summed.reshape(2, half, col_tiles * R)
    lhs = jnp.stack([
        jnp.concatenate([summed[0], -summed[1]], axis=1),
        jnp.concatenate([summed[1], summed[0]], axis=1),
    ])
    y = contract("xvq,mq->xvm", lhs, u_rows)
    residual = y - target

    grad2 = adjoint(residual)
    update2 = first - step_size * to_time(all_freq(grad2))
    threshold2 = threshold_of(update2)
    mine = lax.dynamic_slice_in_dim(update2, freq_pos * times_here, times_here, axis=0)
    mine = mine - jnp.clip(mine, -threshold2, threshold2)
    mine = mine.reshape(times_here, 2, quarter, 2, rows_v)
    own = mine[:, :, :, 0]
    other = swap(mine[:, :, :, 1])
    first_b = jnp.where(core == 0, own, other)
    second_b = jnp.where(core == 0, other, own)
    estimate = jnp.stack([first_b, second_b], axis=2).transpose(4, 0, 1, 2, 3)
    estimate = estimate.reshape(rows_v, times_here * sources)

    res_own = residual[:, :, :rows_u]
    res_other = swap(residual[:, :, rows_u:])
    lo = jnp.where(core == 0, res_own, res_other)
    hi = jnp.where(core == 0, res_other, res_own)
    residual_out = jnp.stack([lo, hi], axis=1).transpose(3, 0, 1, 2).reshape(1, rows_u, 2 * sources)
    return (estimate, residual_out)


def solution(mesh):
    placed = (
        P("freq", "tile", None),
        P(None, "freq", "tile", None),
        P(None, "freq", "tile", None),
        P("freq", None, None),
    )
    return jax.shard_map(
        local,
        mesh=mesh,
        in_specs=placed,
        out_specs=(P("tile", "freq"), P("freq", "tile", None)),
        check_vma=False,
    )
```

```python
import math

import jax
import jax.numpy as jnp
from jax import lax
from jax.sharding import PartitionSpec as P

R = 64
TIMES = 16

step_size = 0.25
shrink_factor = 0.5
energy_floor = 1e-06
highest = lax.Precision.HIGHEST


def contract(form, left, right):
    return jnp.einsum(form, left, right, precision=highest)


def phases(freq_index, time_index, total_times):
    turn_count = (2 * freq_index[:, None] + 1) * time_index[None, :] % total_times
    angle_rad = turn_count.astype(jnp.float32) * (2.0 * math.pi / total_times)
    weight = 1.0 / math.sqrt(total_times)
    return (jnp.cos(angle_rad) * weight, jnp.sin(angle_rad) * weight)


def local(observed, factor_u, factor_v, tile_ranks):
    tile_count = lax.axis_size("tile")
    freq_count = lax.axis_size("freq")
    position = lax.axis_index("tile")
    freq_pos = lax.axis_index("freq")
    core = position % 2
    column = position // 2
    rows_u = factor_u.shape[2]
    rows_v = factor_v.shape[2]
    row_tiles = factor_v.shape[3] // R
    col_tiles = factor_u.shape[3] // R
    sources = observed.shape[2] // 2
    half = sources // 2
    quarter = half // 2
    chips_per_row_tile = tile_count // row_tiles // 2
    times_here = TIMES // freq_count
    total_times = times_here * freq_count
    entries = rows_v * tile_count * total_times * sources
    chunk = (quarter, 2 * R)

    pair = [(k, k ^ 1) for k in range(tile_count)]

    def swap(x):
        return lax.ppermute(x, "tile", pair)

    u_own = factor_u[:, 0]
    v_own = factor_v[:, 0]
    obs_own = observed[0]
    u_both = jnp.concatenate([u_own, swap(u_own)], axis=1)
    v_both = jnp.concatenate([v_own, swap(v_own)], axis=1)
    obs_both = jnp.concatenate([obs_own, swap(obs_own)], axis=0)
    obs_split = obs_both.reshape(2 * rows_u, 2, 2, half)
    target = lax.dynamic_index_in_dim(obs_split, core, axis=2, keepdims=False).transpose(2, 1, 0)

    def weights(f_both, rows, tiles):
        split = f_both.reshape(2, rows, tiles, R).transpose(2, 0, 1, 3)
        real, imag = split[:, 0], split[:, 1]
        top = jnp.stack([real, imag], axis=1)
        bottom = jnp.stack([-imag, real], axis=1)
        return jnp.stack([top, bottom], axis=3).reshape(tiles, 2 * rows, 2 * R)

    w_u = weights(u_both, 2 * rows_u, col_tiles)
    w_v = weights(v_both, 2 * rows_v, row_tiles)

    rank_column = lax.dynamic_index_in_dim(tile_ranks[0], column, axis=1, keepdims=False)
    rank_mask = (jnp.arange(R, dtype=jnp.int32)[None, :] < rank_column[:, None]).astype(jnp.float32)
    rank_mask = jnp.concatenate([rank_mask, rank_mask], axis=1)

    all_freqs = jnp.arange(freq_count, dtype=jnp.int32)
    all_times = jnp.arange(total_times, dtype=jnp.int32)
    cos_tab, sin_tab = phases(all_freqs, all_times, total_times)

    def adjoint(resid):
        lhs = resid.reshape(half, 2 * 2 * rows_u)
        e = contract("vq,jqo->jvo", lhs, w_u)
        outgoing = e.reshape((tile_count,) + chunk)
        incoming = lax.all_to_all(outgoing, "tile", 0, 0, tiled=True)
        gathered = incoming.reshape((row_tiles, chips_per_row_tile, 2) + chunk).sum(axis=1)
        gathered = gathered.reshape(row_tiles, half, 2 * R) * rank_mask[:, None, :]
        blocks = contract("ivo,iqo->ivq", gathered, w_v).sum(axis=0)
        return blocks.reshape(half, 2, 2 * rows_v)

    def all_freq(spectrum):
        outgoing = jnp.broadcast_to(spectrum[None], (freq_count,) + spectrum.shape)
        return lax.all_to_all(outgoing, "freq", 0, 0, tiled=True)

    def to_time(spectra):
        total = 0.0
        for f in range(freq_count):
            total = total + (
                cos_tab[f][:, None, None] * spectra[f, :, 0][None]
                - sin_tab[f][:, None, None] * spectra[f, :, 1][None]
            )
        return total

    def threshold_of(update):
        energy = jnp.sum(update * update)
        outgoing = jnp.broadcast_to(energy, (tile_count, 1))
        total = jnp.sum(lax.all_to_all(outgoing, "tile", 0, 0, tiled=True))
        return shrink_factor * jnp.sqrt(total / entries + energy_floor)

    grad1 = adjoint(target)
    update1 = step_size * to_time(all_freq(grad1))
    threshold1 = threshold_of(update1)
    first = update1 - jnp.clip(update1, -threshold1, threshold1)

    cos_q = lax.dynamic_index_in_dim(cos_tab, freq_pos, axis=0, keepdims=False)
    sin_q = lax.dynamic_index_in_dim(sin_tab, freq_pos, axis=0, keepdims=False)
    x_re = jnp.sum(cos_q[:, None, None] * first, axis=0)
    x_im = -jnp.sum(sin_q[:, None, None] * first, axis=0)
    lhs = jnp.stack([x_re, x_im], axis=1).reshape(half, 2 * 2 * rows_v)
    coeffs = contract("vq,iqo->ivo", lhs, w_v) * rank_mask[:, None, :]
    outgoing = jnp.broadcast_to(
        coeffs.reshape((row_tiles, 1, 2) + chunk),
        (row_tiles, chips_per_row_tile, 2) + chunk,
    ).reshape((tile_count,) + chunk)
    incoming = lax.all_to_all(outgoing, "tile", 0, 0, tiled=True)
    summed = incoming.reshape(col_tiles, half, 2 * R)
    y = contract("jvo,jqo->jvq", summed, w_u).sum(axis=0)
    residual = y.reshape(half, 2, 2 * rows_u) - target

    grad2 = adjoint(residual)
    update2 = first - step_size * to_time(all_freq(grad2))
    threshold2 = threshold_of(update2)
    mine = lax.dynamic_slice_in_dim(update2, freq_pos * times_here, times_here, axis=0)
    mine = mine - jnp.clip(mine, -threshold2, threshold2)
    mine = mine.reshape(times_here, 2, quarter, 2, rows_v)
    own = mine[:, :, :, 0]
    other = swap(mine[:, :, :, 1])
    first_b = jnp.where(core == 0, own, other)
    second_b = jnp.where(core == 0, other, own)
    estimate = jnp.stack([first_b, second_b], axis=2).transpose(4, 0, 1, 2, 3)
    estimate = estimate.reshape(rows_v, times_here * sources)

    res_own = residual[:, :, :rows_u]
    res_other = swap(residual[:, :, rows_u:])
    lo = jnp.where(core == 0, res_own, res_other)
    hi = jnp.where(core == 0, res_other, res_own)
    residual_out = jnp.stack([lo, hi]).transpose(3, 2, 0, 1).reshape(1, rows_u, 2 * sources)
    return (estimate, residual_out)


def solution(mesh):
    placed = (
        P("freq", "tile", None),
        P(None, "freq", "tile", None),
        P(None, "freq", "tile", None),
        P("freq", None, None),
    )
    return jax.shard_map(
        local,
        mesh=mesh,
        in_specs=placed,
        out_specs=(P("tile", "freq"), P("freq", "tile", None)),
        check_vma=False,
    )
```

```python
import math

import jax
import jax.numpy as jnp
from jax import lax
from jax.sharding import PartitionSpec as P

R = 64
TIMES = 16
LANES = 128

step_size = 0.25
shrink_factor = 0.5
energy_floor = 1e-06
matmul_precision = lax.Precision.HIGH


def contract(form, left, right):
    return jnp.einsum(form, left, right, precision=matmul_precision)


def phases(freq_index, time_index, total_times):
    turn_count = (2 * freq_index[:, None] + 1) * time_index[None, :] % total_times
    angle_rad = turn_count.astype(jnp.float32) * (2.0 * math.pi / total_times)
    weight = 1.0 / math.sqrt(total_times)
    return (jnp.cos(angle_rad) * weight, jnp.sin(angle_rad) * weight)


def local(observed, factor_u, factor_v, tile_ranks):
    tile_count = lax.axis_size("tile")
    freq_count = lax.axis_size("freq")
    position = lax.axis_index("tile")
    freq_pos = lax.axis_index("freq")
    core = position % 2
    column = position // 2
    rows_u = factor_u.shape[2]
    rows_v = factor_v.shape[2]
    row_tiles = factor_v.shape[3] // R
    col_tiles = factor_u.shape[3] // R
    sources = observed.shape[2] // 2
    half = sources // 2
    quarter = half // 2
    chips_per_row_tile = tile_count // row_tiles // 2
    times_here = TIMES // freq_count
    total_times = times_here * freq_count
    entries = rows_v * tile_count * total_times * sources
    chunk = (2 * quarter * R // LANES, LANES)

    pair = [(k, k ^ 1) for k in range(tile_count)]

    def swap(x):
        return lax.ppermute(x, "tile", pair)

    u_own = factor_u[:, 0]
    v_own = factor_v[:, 0]
    obs_own = observed[0]
    u_other = swap(u_own)
    u_both = jnp.concatenate([u_own, u_other], axis=1)
    v_both = jnp.concatenate([v_own, swap(v_own)], axis=1)
    obs_both = jnp.concatenate([obs_own, swap(obs_own)], axis=0)
    obs_split = obs_both.reshape(2 * rows_u, 2, 2, half)
    target = lax.dynamic_index_in_dim(obs_split, core, axis=2, keepdims=False).transpose(1, 2, 0)

    rank_column = lax.dynamic_index_in_dim(tile_ranks[0], column, axis=1, keepdims=False)
    rank_mask = (jnp.arange(R, dtype=jnp.int32)[None, :] < rank_column[:, None]).astype(jnp.float32)

    all_freqs = jnp.arange(freq_count, dtype=jnp.int32)
    all_times = jnp.arange(total_times, dtype=jnp.int32)
    cos_tab, sin_tab = phases(all_freqs, all_times, total_times)

    def adjoint(resid, split_rows=False):
        if split_rows:
            products = contract("dvm,cmk->dcvk", resid[:, :, :rows_u], u_own) + contract(
                "dvm,cmk->dcvk", resid[:, :, rows_u:], u_other
            )
        else:
            products = contract("dvm,cmk->dcvk", resid, u_both)
        e_re = products[0, 0] + products[1, 1]
        e_im = products[1, 0] - products[0, 1]
        e = jnp.stack([e_re, e_im]).reshape(2, 2, quarter, col_tiles, R)
        outgoing = e.transpose(3, 1, 0, 2, 4).reshape((tile_count,) + chunk)
        incoming = lax.all_to_all(outgoing, "tile", 0, 0, tiled=True)
        gathered = incoming.reshape((row_tiles, chips_per_row_tile, 2) + chunk).sum(axis=1)
        gathered = gathered.reshape(row_tiles, 2, 2, quarter, R) * rank_mask[:, None, None, None, :]
        coeffs = gathered.transpose(2, 1, 3, 0, 4).reshape(2, half, row_tiles * R)
        blocks = contract("dvk,cnk->dcvn", coeffs, v_both)
        g_re = blocks[0, 0] - blocks[1, 1]
        g_im = blocks[1, 0] + blocks[0, 1]
        return jnp.stack([g_re, g_im])

    def all_freq(spectrum):
        outgoing = jnp.broadcast_to(spectrum[None], (freq_count,) + spectrum.shape)
        return lax.all_to_all(outgoing, "freq", 0, 0, tiled=True)

    def to_time(spectra):
        total = 0.0
        for f in range(freq_count):
            total = total + (
                cos_tab[f][:, None, None] * spectra[f, 0][None]
                - sin_tab[f][:, None, None] * spectra[f, 1][None]
            )
        return total

    def threshold_of(update):
        energy = jnp.sum(update * update)
        outgoing = jnp.broadcast_to(energy, (tile_count, 1))
        total = jnp.sum(lax.all_to_all(outgoing, "tile", 0, 0, tiled=True))
        return shrink_factor * jnp.sqrt(total / entries + energy_floor)

    grad1 = adjoint(target, split_rows=True)
    update1 = step_size * to_time(all_freq(grad1))
    threshold1 = threshold_of(update1)
    first = update1 - jnp.clip(update1, -threshold1, threshold1)

    cos_q = lax.dynamic_index_in_dim(cos_tab, freq_pos, axis=0, keepdims=False)
    sin_q = lax.dynamic_index_in_dim(sin_tab, freq_pos, axis=0, keepdims=False)
    x_re = jnp.sum(cos_q[:, None, None] * first, axis=0)
    x_im = -jnp.sum(sin_q[:, None, None] * first, axis=0)
    products = contract("dvn,cnk->dcvk", jnp.stack([x_re, x_im]), v_both)
    c_re = products[0, 0] + products[1, 1]
    c_im = products[1, 0] - products[0, 1]
    coeffs = jnp.stack([c_re, c_im]).reshape(2, 2, quarter, row_tiles, R)
    coeffs = coeffs * rank_mask[None, None, None, :, :]
    outgoing = jnp.broadcast_to(
        coeffs.transpose(3, 1, 0, 2, 4)[:, None],
        (row_tiles, chips_per_row_tile, 2, 2, quarter, R),
    ).reshape((tile_count,) + chunk)
    incoming = lax.all_to_all(outgoing, "tile", 0, 0, tiled=True)
    summed = incoming.reshape(col_tiles, 2, 2, quarter, R).transpose(2, 1, 3, 0, 4)
    summed = summed.reshape(2, half, col_tiles * R)
    blocks = contract("dvk,cmk->dcvm", summed, u_both)
    y_re = blocks[0, 0] - blocks[1, 1]
    y_im = blocks[1, 0] + blocks[0, 1]
    residual = jnp.stack([y_re, y_im]) - target

    grad2 = adjoint(residual)
    update2 = first - step_size * to_time(all_freq(grad2))
    threshold2 = threshold_of(update2)
    mine = lax.dynamic_slice_in_dim(update2, freq_pos * times_here, times_here, axis=0)
    mine = mine - jnp.clip(mine, -threshold2, threshold2)
    mine = mine.reshape(times_here, 2, quarter, 2, rows_v)
    own = mine[:, :, :, 0]
    other = swap(mine[:, :, :, 1])
    first_b = jnp.where(core == 0, own, other)
    second_b = jnp.where(core == 0, other, own)
    estimate = jnp.stack([first_b, second_b], axis=2).transpose(4, 0, 1, 2, 3)
    estimate = estimate.reshape(rows_v, times_here * sources)

    res_own = residual[:, :, :rows_u]
    res_other = swap(residual[:, :, rows_u:])
    lo = jnp.where(core == 0, res_own, res_other)
    hi = jnp.where(core == 0, res_other, res_own)
    residual_out = jnp.stack([lo, hi], axis=1).transpose(3, 0, 1, 2).reshape(1, rows_u, 2 * sources)
    return (estimate, residual_out)


def solution(mesh):
    placed = (
        P("freq", "tile", None),
        P(None, "freq", "tile", None),
        P(None, "freq", "tile", None),
        P("freq", None, None),
    )
    return jax.shard_map(
        local,
        mesh=mesh,
        in_specs=placed,
        out_specs=(P("tile", "freq"), P("freq", "tile", None)),
        check_vma=False,
    )
```

```python
import math

import jax
import jax.numpy as jnp
from jax import lax
from jax.sharding import PartitionSpec as P

R = 64
TIMES = 16

step_size = 0.25
shrink_factor = 0.5
energy_floor = 1e-06
matmul_precision = lax.Precision.HIGH


def contract(form, left, right):
    return jnp.einsum(form, left, right, precision=matmul_precision)


def phases(freq_index, time_index, total_times):
    turn_count = (2 * freq_index[:, None] + 1) * time_index[None, :] % total_times
    angle_rad = turn_count.astype(jnp.float32) * (2.0 * math.pi / total_times)
    weight = 1.0 / math.sqrt(total_times)
    return (jnp.cos(angle_rad) * weight, jnp.sin(angle_rad) * weight)


def local(observed, factor_u, factor_v, tile_ranks):
    tile_count = lax.axis_size("tile")
    freq_count = lax.axis_size("freq")
    position = lax.axis_index("tile")
    freq_pos = lax.axis_index("freq")
    core = position % 2
    column = position // 2
    rows_u = factor_u.shape[2]
    rows_v = factor_v.shape[2]
    row_tiles = factor_v.shape[3] // R
    col_tiles = factor_u.shape[3] // R
    sources = observed.shape[2] // 2
    half = sources // 2
    quarter = half // 2
    chips_per_row_tile = tile_count // row_tiles // 2
    times_here = TIMES // freq_count
    total_times = times_here * freq_count
    entries = rows_v * tile_count * total_times * sources
    chunk = (quarter, 2 * R)

    pair = [(k, k ^ 1) for k in range(tile_count)]

    def swap(x):
        return lax.ppermute(x, "tile", pair)

    u_own = factor_u[:, 0]
    v_own = factor_v[:, 0]
    obs_own = observed[0]
    u_both = jnp.concatenate([u_own, swap(u_own)], axis=1)
    v_both = jnp.concatenate([v_own, swap(v_own)], axis=1)
    obs_both = jnp.concatenate([obs_own, swap(obs_own)], axis=0)
    obs_split = obs_both.reshape(2 * rows_u, 2, 2, half)
    target = lax.dynamic_index_in_dim(obs_split, core, axis=2, keepdims=False).transpose(2, 1, 0)

    def weights(f_both, rows, tiles):
        split = f_both.reshape(2, rows, tiles, R).transpose(2, 0, 1, 3)
        real, imag = split[:, 0], split[:, 1]
        left = jnp.concatenate([real, imag], axis=1)
        right = jnp.concatenate([-imag, real], axis=1)
        return jnp.concatenate([left, right], axis=2)

    w_u = weights(u_both, 2 * rows_u, col_tiles)
    w_v = weights(v_both, 2 * rows_v, row_tiles)

    rank_column = lax.dynamic_index_in_dim(tile_ranks[0], column, axis=1, keepdims=False)
    rank_mask = (jnp.arange(R, dtype=jnp.int32)[None, :] < rank_column[:, None]).astype(jnp.float32)
    rank_mask = jnp.concatenate([rank_mask, rank_mask], axis=1)

    all_freqs = jnp.arange(freq_count, dtype=jnp.int32)
    all_times = jnp.arange(total_times, dtype=jnp.int32)
    cos_tab, sin_tab = phases(all_freqs, all_times, total_times)

    def adjoint(resid):
        lhs = resid.reshape(half, 2 * 2 * rows_u)
        e = contract("vq,jqo->jvo", lhs, w_u)
        outgoing = e.reshape((tile_count,) + chunk)
        incoming = lax.all_to_all(outgoing, "tile", 0, 0, tiled=True)
        gathered = incoming.reshape((row_tiles, chips_per_row_tile, 2) + chunk).sum(axis=1)
        gathered = gathered.reshape(row_tiles, half, 2 * R) * rank_mask[:, None, :]
        blocks = contract("ivo,iqo->ivq", gathered, w_v).sum(axis=0)
        return blocks.reshape(half, 2, 2 * rows_v)

    def all_freq(spectrum):
        outgoing = jnp.broadcast_to(spectrum[None], (freq_count,) + spectrum.shape)
        return lax.all_to_all(outgoing, "freq", 0, 0, tiled=True)

    def to_time(spectra):
        total = 0.0
        for f in range(freq_count):
            total = total + (
                cos_tab[f][:, None, None] * spectra[f, :, 0][None]
                - sin_tab[f][:, None, None] * spectra[f, :, 1][None]
            )
        return total

    def threshold_of(update):
        energy = jnp.sum(update * update)
        outgoing = jnp.broadcast_to(energy, (tile_count, 1))
        total = jnp.sum(lax.all_to_all(outgoing, "tile", 0, 0, tiled=True))
        return shrink_factor * jnp.sqrt(total / entries + energy_floor)

    grad1 = adjoint(target)
    update1 = step_size * to_time(all_freq(grad1))
    threshold1 = threshold_of(update1)
    first = update1 - jnp.clip(update1, -threshold1, threshold1)

    cos_q = lax.dynamic_index_in_dim(cos_tab, freq_pos, axis=0, keepdims=False)
    sin_q = lax.dynamic_index_in_dim(sin_tab, freq_pos, axis=0, keepdims=False)
    x_re = jnp.sum(cos_q[:, None, None] * first, axis=0)
    x_im = -jnp.sum(sin_q[:, None, None] * first, axis=0)
    lhs = jnp.stack([x_re, x_im], axis=1).reshape(half, 2 * 2 * rows_v)
    coeffs = contract("vq,iqo->ivo", lhs, w_v) * rank_mask[:, None, :]
    outgoing = jnp.broadcast_to(
        coeffs.reshape((row_tiles, 1, 2) + chunk),
        (row_tiles, chips_per_row_tile, 2) + chunk,
    ).reshape((tile_count,) + chunk)
    incoming = lax.all_to_all(outgoing, "tile", 0, 0, tiled=True)
    summed = incoming.reshape(col_tiles, half, 2 * R)
    y = contract("jvo,jqo->jvq", summed, w_u).sum(axis=0)
    residual = y.reshape(half, 2, 2 * rows_u) - target

    grad2 = adjoint(residual)
    update2 = first - step_size * to_time(all_freq(grad2))
    threshold2 = threshold_of(update2)
    mine = lax.dynamic_slice_in_dim(update2, freq_pos * times_here, times_here, axis=0)
    mine = mine - jnp.clip(mine, -threshold2, threshold2)
    mine = mine.reshape(times_here, 2, quarter, 2, rows_v)
    own = mine[:, :, :, 0]
    other = swap(mine[:, :, :, 1])
    first_b = jnp.where(core == 0, own, other)
    second_b = jnp.where(core == 0, other, own)
    estimate = jnp.stack([first_b, second_b], axis=2).transpose(4, 0, 1, 2, 3)
    estimate = estimate.reshape(rows_v, times_here * sources)

    res_own = residual[:, :, :rows_u]
    res_other = swap(residual[:, :, rows_u:])
    lo = jnp.where(core == 0, res_own, res_other)
    hi = jnp.where(core == 0, res_other, res_own)
    residual_out = jnp.stack([lo, hi]).transpose(3, 2, 0, 1).reshape(1, rows_u, 2 * sources)
    return (estimate, residual_out)


def solution(mesh):
    placed = (
        P("freq", "tile", None),
        P(None, "freq", "tile", None),
        P(None, "freq", "tile", None),
        P("freq", None, None),
    )
    return jax.shard_map(
        local,
        mesh=mesh,
        in_specs=placed,
        out_specs=(P("tile", "freq"), P("freq", "tile", None)),
        check_vma=False,
    )
```

```python
import math

import jax
import jax.numpy as jnp
from jax import lax
from jax.sharding import PartitionSpec as P

R = 64
TIMES = 16

step_size = 0.25
shrink_factor = 0.5
energy_floor = 1e-06
matmul_precision = lax.Precision.HIGH


def contract(form, left, right):
    return jnp.einsum(form, left, right, precision=matmul_precision)


def phases(freq_index, time_index, total_times):
    turn_count = (2 * freq_index[:, None] + 1) * time_index[None, :] % total_times
    angle_rad = turn_count.astype(jnp.float32) * (2.0 * math.pi / total_times)
    weight = 1.0 / math.sqrt(total_times)
    return (jnp.cos(angle_rad) * weight, jnp.sin(angle_rad) * weight)


def local(observed, factor_u, factor_v, tile_ranks):
    tile_count = lax.axis_size("tile")
    freq_count = lax.axis_size("freq")
    position = lax.axis_index("tile")
    freq_pos = lax.axis_index("freq")
    core = position % 2
    column = position // 2
    rows_u = factor_u.shape[2]
    rows_v = factor_v.shape[2]
    row_tiles = factor_v.shape[3] // R
    col_tiles = factor_u.shape[3] // R
    sources = observed.shape[2] // 2
    half = sources // 2
    quarter = half // 2
    chips_per_row_tile = tile_count // row_tiles // 2
    times_here = TIMES // freq_count
    total_times = times_here * freq_count
    entries = rows_v * tile_count * total_times * sources
    chunk = (quarter, 2 * R)

    pair = [(k, k ^ 1) for k in range(tile_count)]

    def swap(x):
        return lax.ppermute(x, "tile", pair)

    u_own = factor_u[:, 0]
    v_own = factor_v[:, 0]
    obs_own = observed[0]
    u_other = swap(u_own)
    u_both = jnp.concatenate([u_own, u_other], axis=1)
    v_own, _ = lax.optimization_barrier((v_own, u_other))
    v_both = jnp.concatenate([v_own, swap(v_own)], axis=1)
    obs_both = jnp.concatenate([obs_own, swap(obs_own)], axis=0)
    obs_split = obs_both.reshape(2 * rows_u, 2, 2, half)
    target = lax.dynamic_index_in_dim(obs_split, core, axis=2, keepdims=False).transpose(2, 1, 0)

    def weights(f_both, rows, tiles):
        split = f_both.reshape(2, rows, tiles, R).transpose(2, 0, 1, 3)
        real, imag = split[:, 0], split[:, 1]
        left = jnp.concatenate([real, imag], axis=1)
        right = jnp.concatenate([-imag, real], axis=1)
        return jnp.concatenate([left, right], axis=2)

    w_u = weights(u_both, 2 * rows_u, col_tiles)
    w_v = weights(v_both, 2 * rows_v, row_tiles)

    rank_column = lax.dynamic_index_in_dim(tile_ranks[0], column, axis=1, keepdims=False)
    rank_mask = (jnp.arange(R, dtype=jnp.int32)[None, :] < rank_column[:, None]).astype(jnp.float32)
    rank_mask = jnp.concatenate([rank_mask, rank_mask], axis=1)

    all_freqs = jnp.arange(freq_count, dtype=jnp.int32)
    all_times = jnp.arange(total_times, dtype=jnp.int32)
    cos_tab, sin_tab = phases(all_freqs, all_times, total_times)

    def adjoint(resid):
        lhs = resid.reshape(half, 2 * 2 * rows_u)
        e = contract("vq,jqo->jvo", lhs, w_u)
        outgoing = e.reshape((tile_count,) + chunk)
        incoming = lax.all_to_all(outgoing, "tile", 0, 0, tiled=True)
        gathered = incoming.reshape((row_tiles, chips_per_row_tile, 2) + chunk).sum(axis=1)
        gathered = gathered.reshape(row_tiles, half, 2 * R) * rank_mask[:, None, :]
        blocks = contract("ivo,iqo->ivq", gathered, w_v).sum(axis=0)
        return blocks.reshape(half, 2, 2 * rows_v)

    def all_freq(spectrum):
        outgoing = jnp.broadcast_to(spectrum[None], (freq_count,) + spectrum.shape)
        return lax.all_to_all(outgoing, "freq", 0, 0, tiled=True)

    def to_time(spectra):
        total = 0.0
        for f in range(freq_count):
            total = total + (
                cos_tab[f][:, None, None] * spectra[f, :, 0][None]
                - sin_tab[f][:, None, None] * spectra[f, :, 1][None]
            )
        return total

    def threshold_of(update):
        energy = jnp.sum(update * update)
        outgoing = jnp.broadcast_to(energy, (tile_count, 1))
        total = jnp.sum(lax.all_to_all(outgoing, "tile", 0, 0, tiled=True))
        return shrink_factor * jnp.sqrt(total / entries + energy_floor)

    grad1 = adjoint(target)
    update1 = step_size * to_time(all_freq(grad1))
    threshold1 = threshold_of(update1)
    first = update1 - jnp.clip(update1, -threshold1, threshold1)

    cos_q = lax.dynamic_index_in_dim(cos_tab, freq_pos, axis=0, keepdims=False)
    sin_q = lax.dynamic_index_in_dim(sin_tab, freq_pos, axis=0, keepdims=False)
    x_re = jnp.sum(cos_q[:, None, None] * first, axis=0)
    x_im = -jnp.sum(sin_q[:, None, None] * first, axis=0)
    lhs = jnp.stack([x_re, x_im], axis=1).reshape(half, 2 * 2 * rows_v)
    coeffs = contract("vq,iqo->ivo", lhs, w_v) * rank_mask[:, None, :]
    outgoing = jnp.broadcast_to(
        coeffs.reshape((row_tiles, 1, 2) + chunk),
        (row_tiles, chips_per_row_tile, 2) + chunk,
    ).reshape((tile_count,) + chunk)
    incoming = lax.all_to_all(outgoing, "tile", 0, 0, tiled=True)
    summed = incoming.reshape(col_tiles, half, 2 * R)
    y = contract("jvo,jqo->jvq", summed, w_u).sum(axis=0)
    residual = y.reshape(half, 2, 2 * rows_u) - target

    grad2 = adjoint(residual)
    update2 = first - step_size * to_time(all_freq(grad2))
    threshold2 = threshold_of(update2)
    mine = lax.dynamic_slice_in_dim(update2, freq_pos * times_here, times_here, axis=0)
    mine = mine - jnp.clip(mine, -threshold2, threshold2)
    mine = mine.reshape(times_here, 2, quarter, 2, rows_v)
    own = mine[:, :, :, 0]
    other = swap(mine[:, :, :, 1])
    first_b = jnp.where(core == 0, own, other)
    second_b = jnp.where(core == 0, other, own)
    estimate = jnp.stack([first_b, second_b], axis=2).transpose(4, 0, 1, 2, 3)
    estimate = estimate.reshape(rows_v, times_here * sources)

    res_own = residual[:, :, :rows_u]
    res_other = swap(residual[:, :, rows_u:])
    lo = jnp.where(core == 0, res_own, res_other)
    hi = jnp.where(core == 0, res_other, res_own)
    residual_out = jnp.stack([lo, hi]).transpose(3, 2, 0, 1).reshape(1, rows_u, 2 * sources)
    return (estimate, residual_out)


def solution(mesh):
    placed = (
        P("freq", "tile", None),
        P(None, "freq", "tile", None),
        P(None, "freq", "tile", None),
        P("freq", None, None),
    )
    return jax.shard_map(
        local,
        mesh=mesh,
        in_specs=placed,
        out_specs=(P("tile", "freq"), P("freq", "tile", None)),
        check_vma=False,
    )
```

```python
import math

import jax
import jax.numpy as jnp
from jax import lax
from jax.sharding import PartitionSpec as P

R = 64
TIMES = 16

step_size = 0.25
shrink_factor = 0.5
energy_floor = 1e-06
matmul_precision = lax.Precision.HIGH


def contract(form, left, right):
    return jnp.einsum(form, left, right, precision=matmul_precision)


def phases(freq_index, time_index, total_times):
    turn_count = (2 * freq_index[:, None] + 1) * time_index[None, :] % total_times
    angle_rad = turn_count.astype(jnp.float32) * (2.0 * math.pi / total_times)
    weight = 1.0 / math.sqrt(total_times)
    return (jnp.cos(angle_rad) * weight, jnp.sin(angle_rad) * weight)


def local(observed, factor_u, factor_v, tile_ranks):
    tile_count = lax.axis_size("tile")
    freq_count = lax.axis_size("freq")
    position = lax.axis_index("tile")
    freq_pos = lax.axis_index("freq")
    core = position % 2
    column = position // 2
    rows_u = factor_u.shape[2]
    rows_v = factor_v.shape[2]
    row_tiles = factor_v.shape[3] // R
    col_tiles = factor_u.shape[3] // R
    sources = observed.shape[2] // 2
    half = sources // 2
    quarter = half // 2
    chips_per_row_tile = tile_count // row_tiles // 2
    times_here = TIMES // freq_count
    total_times = times_here * freq_count
    entries = rows_v * tile_count * total_times * sources
    chunk = (quarter, 2 * R)

    pair = [(k, k ^ 1) for k in range(tile_count)]

    def swap(x):
        return lax.ppermute(x, "tile", pair)

    u_own = factor_u[:, 0]
    v_own = factor_v[:, 0]
    obs_own = observed[0]
    u_other = swap(u_own)
    u_both = jnp.concatenate([u_own, u_other], axis=1)
    v_own, _ = lax.optimization_barrier((v_own, u_other))
    v_both = jnp.concatenate([v_own, swap(v_own)], axis=1)
    obs_both = jnp.concatenate([obs_own, swap(obs_own)], axis=0)
    obs_split = obs_both.reshape(2 * rows_u, 2, 2, half)
    target = lax.dynamic_index_in_dim(obs_split, core, axis=2, keepdims=False).transpose(2, 1, 0)

    def weights(f_both, rows, tiles):
        split = f_both.reshape(2, rows, tiles, R).transpose(2, 0, 1, 3)
        real, imag = split[:, 0], split[:, 1]
        left = jnp.concatenate([real, imag], axis=1)
        right = jnp.concatenate([-imag, real], axis=1)
        return jnp.concatenate([left, right], axis=2)

    w_u = weights(u_both, 2 * rows_u, col_tiles)
    w_v = weights(v_both, 2 * rows_v, row_tiles)

    rank_column = lax.dynamic_index_in_dim(tile_ranks[0], column, axis=1, keepdims=False)
    rank_mask = (jnp.arange(R, dtype=jnp.int32)[None, :] < rank_column[:, None]).astype(jnp.float32)
    rank_mask = jnp.concatenate([rank_mask, rank_mask], axis=1)

    all_freqs = jnp.arange(freq_count, dtype=jnp.int32)
    all_times = jnp.arange(total_times, dtype=jnp.int32)
    cos_tab, sin_tab = phases(all_freqs, all_times, total_times)

    def adjoint(resid, direct=False):
        if direct:
            products = contract("vdm,cmk->dcvk", resid[:, :, :rows_u], u_own) + contract(
                "vdm,cmk->dcvk", resid[:, :, rows_u:], u_other
            )
            e = jnp.stack([products[0, 0] + products[1, 1], products[1, 0] - products[0, 1]], axis=1)
            e = e.reshape(2, quarter, 2, col_tiles, R).transpose(3, 0, 1, 2, 4)
        else:
            lhs = resid.reshape(half, 2 * 2 * rows_u)
            e = contract("vq,jqo->jvo", lhs, w_u)
        outgoing = e.reshape((tile_count,) + chunk)
        incoming = lax.all_to_all(outgoing, "tile", 0, 0, tiled=True)
        gathered = incoming.reshape((row_tiles, chips_per_row_tile, 2) + chunk).sum(axis=1)
        gathered = gathered.reshape(row_tiles, half, 2 * R) * rank_mask[:, None, :]
        blocks = contract("ivo,iqo->ivq", gathered, w_v).sum(axis=0)
        return blocks.reshape(half, 2, 2 * rows_v)

    def all_freq(spectrum):
        outgoing = jnp.broadcast_to(spectrum[None], (freq_count,) + spectrum.shape)
        return lax.all_to_all(outgoing, "freq", 0, 0, tiled=True)

    def to_time(spectra):
        total = 0.0
        for f in range(freq_count):
            total = total + (
                cos_tab[f][:, None, None] * spectra[f, :, 0][None]
                - sin_tab[f][:, None, None] * spectra[f, :, 1][None]
            )
        return total

    def threshold_of(update):
        energy = jnp.sum(update * update)
        outgoing = jnp.broadcast_to(energy, (tile_count, 1))
        total = jnp.sum(lax.all_to_all(outgoing, "tile", 0, 0, tiled=True))
        return shrink_factor * jnp.sqrt(total / entries + energy_floor)

    grad1 = adjoint(target, direct=True)
    update1 = step_size * to_time(all_freq(grad1))
    threshold1 = threshold_of(update1)
    first = update1 - jnp.clip(update1, -threshold1, threshold1)

    cos_q = lax.dynamic_index_in_dim(cos_tab, freq_pos, axis=0, keepdims=False)
    sin_q = lax.dynamic_index_in_dim(sin_tab, freq_pos, axis=0, keepdims=False)
    x_re = jnp.sum(cos_q[:, None, None] * first, axis=0)
    x_im = -jnp.sum(sin_q[:, None, None] * first, axis=0)
    lhs = jnp.stack([x_re, x_im], axis=1).reshape(half, 2 * 2 * rows_v)
    coeffs = contract("vq,iqo->ivo", lhs, w_v) * rank_mask[:, None, :]
    outgoing = jnp.broadcast_to(
        coeffs.reshape((row_tiles, 1, 2) + chunk),
        (row_tiles, chips_per_row_tile, 2) + chunk,
    ).reshape((tile_count,) + chunk)
    incoming = lax.all_to_all(outgoing, "tile", 0, 0, tiled=True)
    summed = incoming.reshape(col_tiles, half, 2 * R)
    y = contract("jvo,jqo->jvq", summed, w_u).sum(axis=0)
    residual = y.reshape(half, 2, 2 * rows_u) - target

    grad2 = adjoint(residual)
    update2 = first - step_size * to_time(all_freq(grad2))
    threshold2 = threshold_of(update2)
    mine = lax.dynamic_slice_in_dim(update2, freq_pos * times_here, times_here, axis=0)
    mine = mine - jnp.clip(mine, -threshold2, threshold2)
    mine = mine.reshape(times_here, 2, quarter, 2, rows_v)
    own = mine[:, :, :, 0]
    other = swap(mine[:, :, :, 1])
    first_b = jnp.where(core == 0, own, other)
    second_b = jnp.where(core == 0, other, own)
    estimate = jnp.stack([first_b, second_b], axis=2).transpose(4, 0, 1, 2, 3)
    estimate = estimate.reshape(rows_v, times_here * sources)

    res_own = residual[:, :, :rows_u]
    res_other = swap(residual[:, :, rows_u:])
    lo = jnp.where(core == 0, res_own, res_other)
    hi = jnp.where(core == 0, res_other, res_own)
    residual_out = jnp.stack([lo, hi]).transpose(3, 2, 0, 1).reshape(1, rows_u, 2 * sources)
    return (estimate, residual_out)


def solution(mesh):
    placed = (
        P("freq", "tile", None),
        P(None, "freq", "tile", None),
        P(None, "freq", "tile", None),
        P("freq", None, None),
    )
    return jax.shard_map(
        local,
        mesh=mesh,
        in_specs=placed,
        out_specs=(P("tile", "freq"), P("freq", "tile", None)),
        check_vma=False,
    )
```

```python
import math

import jax
import jax.numpy as jnp
from jax import lax
from jax.experimental import pallas as pl
from jax.sharding import PartitionSpec as P

R = 64
TIMES = 16

step_size = 0.25
shrink_factor = 0.5
energy_floor = 1e-06
matmul_precision = lax.Precision.HIGH


def contract(form, left, right):
    return jnp.einsum(form, left, right, precision=matmul_precision)


def phases(freq_index, time_index, total_times):
    turn_count = (2 * freq_index[:, None] + 1) * time_index[None, :] % total_times
    angle_rad = turn_count.astype(jnp.float32) * (2.0 * math.pi / total_times)
    weight = 1.0 / math.sqrt(total_times)
    return (jnp.cos(angle_rad) * weight, jnp.sin(angle_rad) * weight)


def weight_kernel(own_ref, other_ref, out_ref):
    for jj in range(2):
        lo, hi = jj * R, (jj + 1) * R
        re = jnp.concatenate([own_ref[0, :, lo:hi], other_ref[0, :, lo:hi]], axis=0)
        im = jnp.concatenate([own_ref[1, :, lo:hi], other_ref[1, :, lo:hi]], axis=0)
        rows = re.shape[0]
        out_ref[jj, :rows, :R] = re
        out_ref[jj, rows:, :R] = im
        out_ref[jj, :rows, R:] = -im
        out_ref[jj, rows:, R:] = re


def build_weights(own, other):
    rows, cols = own.shape[1], own.shape[2]
    tiles = cols // R
    spec = pl.BlockSpec((2, rows, 2 * R), lambda p: (0, 0, p))
    return pl.pallas_call(
        weight_kernel,
        grid=(tiles // 2,),
        in_specs=[spec, spec],
        out_specs=pl.BlockSpec((2, 4 * rows, 2 * R), lambda p: (p, 0, 0)),
        out_shape=jax.ShapeDtypeStruct((tiles, 4 * rows, 2 * R), own.dtype),
    )(own, other)


def local(observed, factor_u, factor_v, tile_ranks):
    tile_count = lax.axis_size("tile")
    freq_count = lax.axis_size("freq")
    position = lax.axis_index("tile")
    freq_pos = lax.axis_index("freq")
    core = position % 2
    column = position // 2
    rows_u = factor_u.shape[2]
    rows_v = factor_v.shape[2]
    row_tiles = factor_v.shape[3] // R
    col_tiles = factor_u.shape[3] // R
    sources = observed.shape[2] // 2
    half = sources // 2
    quarter = half // 2
    chips_per_row_tile = tile_count // row_tiles // 2
    times_here = TIMES // freq_count
    total_times = times_here * freq_count
    entries = rows_v * tile_count * total_times * sources
    chunk = (quarter, 2 * R)

    pair = [(k, k ^ 1) for k in range(tile_count)]

    def swap(x):
        return lax.ppermute(x, "tile", pair)

    u_own = factor_u[:, 0]
    v_own = factor_v[:, 0]
    obs_own = observed[0]
    u_other = swap(u_own)
    v_own, _ = lax.optimization_barrier((v_own, u_other))
    v_other = swap(v_own)
    obs_both = jnp.concatenate([obs_own, swap(obs_own)], axis=0)
    obs_split = obs_both.reshape(2 * rows_u, 2, 2, half)
    target = lax.dynamic_index_in_dim(obs_split, core, axis=2, keepdims=False).transpose(2, 1, 0)

    w_u = build_weights(u_own, u_other)
    w_v = build_weights(v_own, v_other)

    rank_column = lax.dynamic_index_in_dim(tile_ranks[0], column, axis=1, keepdims=False)
    rank_mask = (jnp.arange(R, dtype=jnp.int32)[None, :] < rank_column[:, None]).astype(jnp.float32)
    rank_mask = jnp.concatenate([rank_mask, rank_mask], axis=1)

    all_freqs = jnp.arange(freq_count, dtype=jnp.int32)
    all_times = jnp.arange(total_times, dtype=jnp.int32)
    cos_tab, sin_tab = phases(all_freqs, all_times, total_times)

    def adjoint(resid):
        lhs = resid.reshape(half, 2 * 2 * rows_u)
        e = contract("vq,jqo->jvo", lhs, w_u)
        outgoing = e.reshape((tile_count,) + chunk)
        incoming = lax.all_to_all(outgoing, "tile", 0, 0, tiled=True)
        gathered = incoming.reshape((row_tiles, chips_per_row_tile, 2) + chunk).sum(axis=1)
        gathered = gathered.reshape(row_tiles, half, 2 * R) * rank_mask[:, None, :]
        blocks = contract("ivo,iqo->ivq", gathered, w_v).sum(axis=0)
        return blocks.reshape(half, 2, 2 * rows_v)

    def all_freq(spectrum):
        outgoing = jnp.broadcast_to(spectrum[None], (freq_count,) + spectrum.shape)
        return lax.all_to_all(outgoing, "freq", 0, 0, tiled=True)

    def to_time(spectra):
        total = 0.0
        for f in range(freq_count):
            total = total + (
                cos_tab[f][:, None, None] * spectra[f, :, 0][None]
                - sin_tab[f][:, None, None] * spectra[f, :, 1][None]
            )
        return total

    def threshold_of(update):
        energy = jnp.sum(update * update)
        outgoing = jnp.broadcast_to(energy, (tile_count, 1))
        total = jnp.sum(lax.all_to_all(outgoing, "tile", 0, 0, tiled=True))
        return shrink_factor * jnp.sqrt(total / entries + energy_floor)

    grad1 = adjoint(target)
    update1 = step_size * to_time(all_freq(grad1))
    threshold1 = threshold_of(update1)
    first = update1 - jnp.clip(update1, -threshold1, threshold1)

    cos_q = lax.dynamic_index_in_dim(cos_tab, freq_pos, axis=0, keepdims=False)
    sin_q = lax.dynamic_index_in_dim(sin_tab, freq_pos, axis=0, keepdims=False)
    x_re = jnp.sum(cos_q[:, None, None] * first, axis=0)
    x_im = -jnp.sum(sin_q[:, None, None] * first, axis=0)
    lhs = jnp.stack([x_re, x_im], axis=1).reshape(half, 2 * 2 * rows_v)
    coeffs = contract("vq,iqo->ivo", lhs, w_v) * rank_mask[:, None, :]
    outgoing = jnp.broadcast_to(
        coeffs.reshape((row_tiles, 1, 2) + chunk),
        (row_tiles, chips_per_row_tile, 2) + chunk,
    ).reshape((tile_count,) + chunk)
    incoming = lax.all_to_all(outgoing, "tile", 0, 0, tiled=True)
    summed = incoming.reshape(col_tiles, half, 2 * R)
    y = contract("jvo,jqo->jvq", summed, w_u).sum(axis=0)
    residual = y.reshape(half, 2, 2 * rows_u) - target

    grad2 = adjoint(residual)
    update2 = first - step_size * to_time(all_freq(grad2))
    threshold2 = threshold_of(update2)
    mine = lax.dynamic_slice_in_dim(update2, freq_pos * times_here, times_here, axis=0)
    mine = mine - jnp.clip(mine, -threshold2, threshold2)
    mine = mine.reshape(times_here, 2, quarter, 2, rows_v)
    own = mine[:, :, :, 0]
    other = swap(mine[:, :, :, 1])
    first_b = jnp.where(core == 0, own, other)
    second_b = jnp.where(core == 0, other, own)
    estimate = jnp.stack([first_b, second_b], axis=2).transpose(4, 0, 1, 2, 3)
    estimate = estimate.reshape(rows_v, times_here * sources)

    res_own = residual[:, :, :rows_u]
    res_other = swap(residual[:, :, rows_u:])
    lo = jnp.where(core == 0, res_own, res_other)
    hi = jnp.where(core == 0, res_other, res_own)
    residual_out = jnp.stack([lo, hi]).transpose(3, 2, 0, 1).reshape(1, rows_u, 2 * sources)
    return (estimate, residual_out)


def solution(mesh):
    placed = (
        P("freq", "tile", None),
        P(None, "freq", "tile", None),
        P(None, "freq", "tile", None),
        P("freq", None, None),
    )
    return jax.shard_map(
        local,
        mesh=mesh,
        in_specs=placed,
        out_specs=(P("tile", "freq"), P("freq", "tile", None)),
        check_vma=False,
    )
```

```python
import math

import jax
import jax.numpy as jnp
from jax import lax
from jax.experimental import pallas as pl
from jax.sharding import PartitionSpec as P

R = 64
TIMES = 16

step_size = 0.25
shrink_factor = 0.5
energy_floor = 1e-06
matmul_precision = lax.Precision.HIGH


def contract(form, left, right):
    return jnp.einsum(form, left, right, precision=matmul_precision)


def phases(freq_index, time_index, total_times):
    turn_count = (2 * freq_index[:, None] + 1) * time_index[None, :] % total_times
    angle_rad = turn_count.astype(jnp.float32) * (2.0 * math.pi / total_times)
    weight = 1.0 / math.sqrt(total_times)
    return (jnp.cos(angle_rad) * weight, jnp.sin(angle_rad) * weight)


def weight_kernel(own_ref, other_ref, out_ref):
    for jj in range(out_ref.shape[0]):
        lo, hi = jj * R, (jj + 1) * R
        re = jnp.concatenate([own_ref[0, :, lo:hi], other_ref[0, :, lo:hi]], axis=0)
        im = jnp.concatenate([own_ref[1, :, lo:hi], other_ref[1, :, lo:hi]], axis=0)
        rows = re.shape[0]
        out_ref[jj, :rows, :R] = re
        out_ref[jj, rows:, :R] = im
        out_ref[jj, :rows, R:] = -im
        out_ref[jj, rows:, R:] = re


def build_weights(own, other):
    rows, cols = own.shape[1], own.shape[2]
    tiles = cols // R
    per_step = min(tiles, 16)
    spec = pl.BlockSpec((2, rows, per_step * R), lambda p: (0, 0, p))
    return pl.pallas_call(
        weight_kernel,
        grid=(tiles // per_step,),
        in_specs=[spec, spec],
        out_specs=pl.BlockSpec((per_step, 4 * rows, 2 * R), lambda p: (p, 0, 0)),
        out_shape=jax.ShapeDtypeStruct((tiles, 4 * rows, 2 * R), own.dtype),
    )(own, other)

def local(observed, factor_u, factor_v, tile_ranks):
    tile_count = lax.axis_size("tile")
    freq_count = lax.axis_size("freq")
    position = lax.axis_index("tile")
    freq_pos = lax.axis_index("freq")
    core = position % 2
    column = position // 2
    rows_u = factor_u.shape[2]
    rows_v = factor_v.shape[2]
    row_tiles = factor_v.shape[3] // R
    col_tiles = factor_u.shape[3] // R
    sources = observed.shape[2] // 2
    half = sources // 2
    quarter = half // 2
    chips_per_row_tile = tile_count // row_tiles // 2
    times_here = TIMES // freq_count
    total_times = times_here * freq_count
    entries = rows_v * tile_count * total_times * sources
    chunk = (quarter, 2 * R)

    pair = [(k, k ^ 1) for k in range(tile_count)]

    def swap(x):
        return lax.ppermute(x, "tile", pair)

    u_own = factor_u[:, 0]
    v_own = factor_v[:, 0]
    obs_own = observed[0]
    u_other = swap(u_own)
    v_own, _ = lax.optimization_barrier((v_own, u_other))
    v_other = swap(v_own)
    obs_both = jnp.concatenate([obs_own, swap(obs_own)], axis=0)
    obs_split = obs_both.reshape(2 * rows_u, 2, 2, half)
    target = lax.dynamic_index_in_dim(obs_split, core, axis=2, keepdims=False).transpose(2, 1, 0)

    w_u = build_weights(u_own, u_other)
    w_v = build_weights(v_own, v_other)

    rank_column = lax.dynamic_index_in_dim(tile_ranks[0], column, axis=1, keepdims=False)
    rank_mask = (jnp.arange(R, dtype=jnp.int32)[None, :] < rank_column[:, None]).astype(jnp.float32)
    rank_mask = jnp.concatenate([rank_mask, rank_mask], axis=1)

    all_freqs = jnp.arange(freq_count, dtype=jnp.int32)
    all_times = jnp.arange(total_times, dtype=jnp.int32)
    cos_tab, sin_tab = phases(all_freqs, all_times, total_times)

    def adjoint(resid):
        lhs = resid.reshape(half, 2 * 2 * rows_u)
        e = contract("vq,jqo->jvo", lhs, w_u)
        outgoing = e.reshape((tile_count,) + chunk)
        incoming = lax.all_to_all(outgoing, "tile", 0, 0, tiled=True)
        gathered = incoming.reshape((row_tiles, chips_per_row_tile, 2) + chunk).sum(axis=1)
        gathered = gathered.reshape(row_tiles, half, 2 * R) * rank_mask[:, None, :]
        blocks = contract("ivo,iqo->ivq", gathered, w_v).sum(axis=0)
        return blocks.reshape(half, 2, 2 * rows_v)

    def all_freq(spectrum):
        outgoing = jnp.broadcast_to(spectrum[None], (freq_count,) + spectrum.shape)
        return lax.all_to_all(outgoing, "freq", 0, 0, tiled=True)

    def to_time(spectra):
        total = 0.0
        for f in range(freq_count):
            total = total + (
                cos_tab[f][:, None, None] * spectra[f, :, 0][None]
                - sin_tab[f][:, None, None] * spectra[f, :, 1][None]
            )
        return total

    def threshold_of(update):
        energy = jnp.sum(update * update)
        outgoing = jnp.broadcast_to(energy, (tile_count, 1))
        total = jnp.sum(lax.all_to_all(outgoing, "tile", 0, 0, tiled=True))
        return shrink_factor * jnp.sqrt(total / entries + energy_floor)

    grad1 = adjoint(target)
    update1 = step_size * to_time(all_freq(grad1))
    threshold1 = threshold_of(update1)
    first = update1 - jnp.clip(update1, -threshold1, threshold1)

    cos_q = lax.dynamic_index_in_dim(cos_tab, freq_pos, axis=0, keepdims=False)
    sin_q = lax.dynamic_index_in_dim(sin_tab, freq_pos, axis=0, keepdims=False)
    x_re = jnp.sum(cos_q[:, None, None] * first, axis=0)
    x_im = -jnp.sum(sin_q[:, None, None] * first, axis=0)
    lhs = jnp.stack([x_re, x_im], axis=1).reshape(half, 2 * 2 * rows_v)
    coeffs = contract("vq,iqo->ivo", lhs, w_v) * rank_mask[:, None, :]
    outgoing = jnp.broadcast_to(
        coeffs.reshape((row_tiles, 1, 2) + chunk),
        (row_tiles, chips_per_row_tile, 2) + chunk,
    ).reshape((tile_count,) + chunk)
    incoming = lax.all_to_all(outgoing, "tile", 0, 0, tiled=True)
    summed = incoming.reshape(col_tiles, half, 2 * R)
    y = contract("jvo,jqo->jvq", summed, w_u).sum(axis=0)
    residual = y.reshape(half, 2, 2 * rows_u) - target

    grad2 = adjoint(residual)
    update2 = first - step_size * to_time(all_freq(grad2))
    threshold2 = threshold_of(update2)
    mine = lax.dynamic_slice_in_dim(update2, freq_pos * times_here, times_here, axis=0)
    mine = mine - jnp.clip(mine, -threshold2, threshold2)
    mine = mine.reshape(times_here, 2, quarter, 2, rows_v)
    own = mine[:, :, :, 0]
    other = swap(mine[:, :, :, 1])
    first_b = jnp.where(core == 0, own, other)
    second_b = jnp.where(core == 0, other, own)
    estimate = jnp.stack([first_b, second_b], axis=2).transpose(4, 0, 1, 2, 3)
    estimate = estimate.reshape(rows_v, times_here * sources)

    res_own = residual[:, :, :rows_u]
    res_other = swap(residual[:, :, rows_u:])
    lo = jnp.where(core == 0, res_own, res_other)
    hi = jnp.where(core == 0, res_other, res_own)
    residual_out = jnp.stack([lo, hi]).transpose(3, 2, 0, 1).reshape(1, rows_u, 2 * sources)
    return (estimate, residual_out)


def solution(mesh):
    placed = (
        P("freq", "tile", None),
        P(None, "freq", "tile", None),
        P(None, "freq", "tile", None),
        P("freq", None, None),
    )
    return jax.shard_map(
        local,
        mesh=mesh,
        in_specs=placed,
        out_specs=(P("tile", "freq"), P("freq", "tile", None)),
        check_vma=False,
    )
```

```python
import math

import jax
import jax.numpy as jnp
from jax import lax
from jax.experimental import pallas as pl
from jax.sharding import PartitionSpec as P

R = 64
TIMES = 16

step_size = 0.25
shrink_factor = 0.5
energy_floor = 1e-06
matmul_precision = lax.Precision.HIGH


def contract(form, left, right):
    return jnp.einsum(form, left, right, precision=matmul_precision)


def phases(freq_index, time_index, total_times):
    turn_count = (2 * freq_index[:, None] + 1) * time_index[None, :] % total_times
    angle_rad = turn_count.astype(jnp.float32) * (2.0 * math.pi / total_times)
    weight = 1.0 / math.sqrt(total_times)
    return (jnp.cos(angle_rad) * weight, jnp.sin(angle_rad) * weight)


def weight_kernel(own_ref, other_ref, out_ref):
    for jj in range(out_ref.shape[0]):
        lo, hi = jj * R, (jj + 1) * R
        re = jnp.concatenate([own_ref[0, :, lo:hi], other_ref[0, :, lo:hi]], axis=0)
        im = jnp.concatenate([own_ref[1, :, lo:hi], other_ref[1, :, lo:hi]], axis=0)
        rows = re.shape[0]
        out_ref[jj, :rows, :R] = re
        out_ref[jj, rows:, :R] = im
        out_ref[jj, :rows, R:] = -im
        out_ref[jj, rows:, R:] = re


def build_weights(own, other):
    rows, cols = own.shape[1], own.shape[2]
    tiles = cols // R
    per_step = min(tiles, 32)
    spec = pl.BlockSpec((2, rows, per_step * R), lambda p: (0, 0, p))
    return pl.pallas_call(
        weight_kernel,
        grid=(tiles // per_step,),
        in_specs=[spec, spec],
        out_specs=pl.BlockSpec((per_step, 4 * rows, 2 * R), lambda p: (p, 0, 0)),
        out_shape=jax.ShapeDtypeStruct((tiles, 4 * rows, 2 * R), own.dtype),
    )(own, other)

def local(observed, factor_u, factor_v, tile_ranks):
    tile_count = lax.axis_size("tile")
    freq_count = lax.axis_size("freq")
    position = lax.axis_index("tile")
    freq_pos = lax.axis_index("freq")
    core = position % 2
    column = position // 2
    rows_u = factor_u.shape[2]
    rows_v = factor_v.shape[2]
    row_tiles = factor_v.shape[3] // R
    col_tiles = factor_u.shape[3] // R
    sources = observed.shape[2] // 2
    half = sources // 2
    quarter = half // 2
    chips_per_row_tile = tile_count // row_tiles // 2
    times_here = TIMES // freq_count
    total_times = times_here * freq_count
    entries = rows_v * tile_count * total_times * sources
    chunk = (quarter, 2 * R)

    pair = [(k, k ^ 1) for k in range(tile_count)]

    def swap(x):
        return lax.ppermute(x, "tile", pair)

    u_own = factor_u[:, 0]
    v_own = factor_v[:, 0]
    obs_own = observed[0]
    u_other = swap(u_own)
    v_own, _ = lax.optimization_barrier((v_own, u_other))
    v_other = swap(v_own)
    obs_both = jnp.concatenate([obs_own, swap(obs_own)], axis=0)
    obs_split = obs_both.reshape(2 * rows_u, 2, 2, half)
    target = lax.dynamic_index_in_dim(obs_split, core, axis=2, keepdims=False).transpose(2, 1, 0)

    w_u = build_weights(u_own, u_other)
    w_v = build_weights(v_own, v_other)

    rank_column = lax.dynamic_index_in_dim(tile_ranks[0], column, axis=1, keepdims=False)
    rank_mask = (jnp.arange(R, dtype=jnp.int32)[None, :] < rank_column[:, None]).astype(jnp.float32)
    rank_mask = jnp.concatenate([rank_mask, rank_mask], axis=1)

    all_freqs = jnp.arange(freq_count, dtype=jnp.int32)
    all_times = jnp.arange(total_times, dtype=jnp.int32)
    cos_tab, sin_tab = phases(all_freqs, all_times, total_times)

    def adjoint(resid):
        lhs = resid.reshape(half, 2 * 2 * rows_u)
        e = contract("vq,jqo->jvo", lhs, w_u)
        outgoing = e.reshape((tile_count,) + chunk)
        incoming = lax.all_to_all(outgoing, "tile", 0, 0, tiled=True)
        gathered = incoming.reshape((row_tiles, chips_per_row_tile, 2) + chunk).sum(axis=1)
        gathered = gathered.reshape(row_tiles, half, 2 * R) * rank_mask[:, None, :]
        blocks = contract("ivo,iqo->ivq", gathered, w_v).sum(axis=0)
        return blocks.reshape(half, 2, 2 * rows_v)

    def all_freq(spectrum):
        outgoing = jnp.broadcast_to(spectrum[None], (freq_count,) + spectrum.shape)
        return lax.all_to_all(outgoing, "freq", 0, 0, tiled=True)

    def to_time(spectra):
        total = 0.0
        for f in range(freq_count):
            total = total + (
                cos_tab[f][:, None, None] * spectra[f, :, 0][None]
                - sin_tab[f][:, None, None] * spectra[f, :, 1][None]
            )
        return total

    def threshold_of(update):
        energy = jnp.sum(update * update)
        outgoing = jnp.broadcast_to(energy, (tile_count, 1))
        total = jnp.sum(lax.all_to_all(outgoing, "tile", 0, 0, tiled=True))
        return shrink_factor * jnp.sqrt(total / entries + energy_floor)

    grad1 = adjoint(target)
    update1 = step_size * to_time(all_freq(grad1))
    threshold1 = threshold_of(update1)
    first = update1 - jnp.clip(update1, -threshold1, threshold1)

    cos_q = lax.dynamic_index_in_dim(cos_tab, freq_pos, axis=0, keepdims=False)
    sin_q = lax.dynamic_index_in_dim(sin_tab, freq_pos, axis=0, keepdims=False)
    x_re = jnp.sum(cos_q[:, None, None] * first, axis=0)
    x_im = -jnp.sum(sin_q[:, None, None] * first, axis=0)
    lhs = jnp.stack([x_re, x_im], axis=1).reshape(half, 2 * 2 * rows_v)
    coeffs = contract("vq,iqo->ivo", lhs, w_v) * rank_mask[:, None, :]
    outgoing = jnp.broadcast_to(
        coeffs.reshape((row_tiles, 1, 2) + chunk),
        (row_tiles, chips_per_row_tile, 2) + chunk,
    ).reshape((tile_count,) + chunk)
    incoming = lax.all_to_all(outgoing, "tile", 0, 0, tiled=True)
    summed = incoming.reshape(col_tiles, half, 2 * R)
    y = contract("jvo,jqo->jvq", summed, w_u).sum(axis=0)
    residual = y.reshape(half, 2, 2 * rows_u) - target

    grad2 = adjoint(residual)
    update2 = first - step_size * to_time(all_freq(grad2))
    threshold2 = threshold_of(update2)
    mine = lax.dynamic_slice_in_dim(update2, freq_pos * times_here, times_here, axis=0)
    mine = mine - jnp.clip(mine, -threshold2, threshold2)
    mine = mine.reshape(times_here, 2, quarter, 2, rows_v)
    own = mine[:, :, :, 0]
    other = swap(mine[:, :, :, 1])
    first_b = jnp.where(core == 0, own, other)
    second_b = jnp.where(core == 0, other, own)
    estimate = jnp.stack([first_b, second_b], axis=2).transpose(4, 0, 1, 2, 3)
    estimate = estimate.reshape(rows_v, times_here * sources)

    res_own = residual[:, :, :rows_u]
    res_other = swap(residual[:, :, rows_u:])
    lo = jnp.where(core == 0, res_own, res_other)
    hi = jnp.where(core == 0, res_other, res_own)
    residual_out = jnp.stack([lo, hi]).transpose(3, 2, 0, 1).reshape(1, rows_u, 2 * sources)
    return (estimate, residual_out)


def solution(mesh):
    placed = (
        P("freq", "tile", None),
        P(None, "freq", "tile", None),
        P(None, "freq", "tile", None),
        P("freq", None, None),
    )
    return jax.shard_map(
        local,
        mesh=mesh,
        in_specs=placed,
        out_specs=(P("tile", "freq"), P("freq", "tile", None)),
        check_vma=False,
    )
```

```python
import math

import jax
import jax.numpy as jnp
from jax import lax
from jax.experimental import pallas as pl
from jax.sharding import PartitionSpec as P

R = 64
TIMES = 16

step_size = 0.25
shrink_factor = 0.5
energy_floor = 1e-06
matmul_precision = lax.Precision.HIGH


def contract(form, left, right):
    return jnp.einsum(form, left, right, precision=matmul_precision)


def phases(freq_index, time_index, total_times):
    turn_count = (2 * freq_index[:, None] + 1) * time_index[None, :] % total_times
    angle_rad = turn_count.astype(jnp.float32) * (2.0 * math.pi / total_times)
    weight = 1.0 / math.sqrt(total_times)
    return (jnp.cos(angle_rad) * weight, jnp.sin(angle_rad) * weight)


def weight_kernel(own_ref, other_ref, out_ref):
    for jj in range(out_ref.shape[0]):
        lo, hi = jj * R, (jj + 1) * R
        re = jnp.concatenate([own_ref[0, :, lo:hi], other_ref[0, :, lo:hi]], axis=0)
        im = jnp.concatenate([own_ref[1, :, lo:hi], other_ref[1, :, lo:hi]], axis=0)
        rows = re.shape[0]
        out_ref[jj, :rows, :R] = re
        out_ref[jj, rows:, :R] = im
        out_ref[jj, :rows, R:] = -im
        out_ref[jj, rows:, R:] = re


def build_weights(own, other):
    rows, cols = own.shape[1], own.shape[2]
    tiles = cols // R
    per_step = tiles
    spec = pl.BlockSpec((2, rows, per_step * R), lambda p: (0, 0, p))
    return pl.pallas_call(
        weight_kernel,
        grid=(tiles // per_step,),
        in_specs=[spec, spec],
        out_specs=pl.BlockSpec((per_step, 4 * rows, 2 * R), lambda p: (p, 0, 0)),
        out_shape=jax.ShapeDtypeStruct((tiles, 4 * rows, 2 * R), own.dtype),
    )(own, other)

def local(observed, factor_u, factor_v, tile_ranks):
    tile_count = lax.axis_size("tile")
    freq_count = lax.axis_size("freq")
    position = lax.axis_index("tile")
    freq_pos = lax.axis_index("freq")
    core = position % 2
    column = position // 2
    rows_u = factor_u.shape[2]
    rows_v = factor_v.shape[2]
    row_tiles = factor_v.shape[3] // R
    col_tiles = factor_u.shape[3] // R
    sources = observed.shape[2] // 2
    half = sources // 2
    quarter = half // 2
    chips_per_row_tile = tile_count // row_tiles // 2
    times_here = TIMES // freq_count
    total_times = times_here * freq_count
    entries = rows_v * tile_count * total_times * sources
    chunk = (quarter, 2 * R)

    pair = [(k, k ^ 1) for k in range(tile_count)]

    def swap(x):
        return lax.ppermute(x, "tile", pair)

    u_own = factor_u[:, 0]
    v_own = factor_v[:, 0]
    obs_own = observed[0]
    u_other = swap(u_own)
    v_own, _ = lax.optimization_barrier((v_own, u_other))
    v_other = swap(v_own)
    obs_both = jnp.concatenate([obs_own, swap(obs_own)], axis=0)
    obs_split = obs_both.reshape(2 * rows_u, 2, 2, half)
    target = lax.dynamic_index_in_dim(obs_split, core, axis=2, keepdims=False).transpose(2, 1, 0)

    w_u = build_weights(u_own, u_other)
    w_v = build_weights(v_own, v_other)

    rank_column = lax.dynamic_index_in_dim(tile_ranks[0], column, axis=1, keepdims=False)
    rank_mask = (jnp.arange(R, dtype=jnp.int32)[None, :] < rank_column[:, None]).astype(jnp.float32)
    rank_mask = jnp.concatenate([rank_mask, rank_mask], axis=1)

    all_freqs = jnp.arange(freq_count, dtype=jnp.int32)
    all_times = jnp.arange(total_times, dtype=jnp.int32)
    cos_tab, sin_tab = phases(all_freqs, all_times, total_times)

    def adjoint(resid):
        lhs = resid.reshape(half, 2 * 2 * rows_u)
        e = contract("vq,jqo->jvo", lhs, w_u)
        outgoing = e.reshape((tile_count,) + chunk)
        incoming = lax.all_to_all(outgoing, "tile", 0, 0, tiled=True)
        gathered = incoming.reshape((row_tiles, chips_per_row_tile, 2) + chunk).sum(axis=1)
        gathered = gathered.reshape(row_tiles, half, 2 * R) * rank_mask[:, None, :]
        blocks = contract("ivo,iqo->ivq", gathered, w_v).sum(axis=0)
        return blocks.reshape(half, 2, 2 * rows_v)

    def all_freq(spectrum):
        outgoing = jnp.broadcast_to(spectrum[None], (freq_count,) + spectrum.shape)
        return lax.all_to_all(outgoing, "freq", 0, 0, tiled=True)

    def to_time(spectra):
        total = 0.0
        for f in range(freq_count):
            total = total + (
                cos_tab[f][:, None, None] * spectra[f, :, 0][None]
                - sin_tab[f][:, None, None] * spectra[f, :, 1][None]
            )
        return total

    def threshold_of(update):
        energy = jnp.sum(update * update)
        outgoing = jnp.broadcast_to(energy, (tile_count, 1))
        total = jnp.sum(lax.all_to_all(outgoing, "tile", 0, 0, tiled=True))
        return shrink_factor * jnp.sqrt(total / entries + energy_floor)

    grad1 = adjoint(target)
    update1 = step_size * to_time(all_freq(grad1))
    threshold1 = threshold_of(update1)
    first = update1 - jnp.clip(update1, -threshold1, threshold1)

    cos_q = lax.dynamic_index_in_dim(cos_tab, freq_pos, axis=0, keepdims=False)
    sin_q = lax.dynamic_index_in_dim(sin_tab, freq_pos, axis=0, keepdims=False)
    x_re = jnp.sum(cos_q[:, None, None] * first, axis=0)
    x_im = -jnp.sum(sin_q[:, None, None] * first, axis=0)
    lhs = jnp.stack([x_re, x_im], axis=1).reshape(half, 2 * 2 * rows_v)
    coeffs = contract("vq,iqo->ivo", lhs, w_v) * rank_mask[:, None, :]
    outgoing = jnp.broadcast_to(
        coeffs.reshape((row_tiles, 1, 2) + chunk),
        (row_tiles, chips_per_row_tile, 2) + chunk,
    ).reshape((tile_count,) + chunk)
    incoming = lax.all_to_all(outgoing, "tile", 0, 0, tiled=True)
    summed = incoming.reshape(col_tiles, half, 2 * R)
    y = contract("jvo,jqo->jvq", summed, w_u).sum(axis=0)
    residual = y.reshape(half, 2, 2 * rows_u) - target

    grad2 = adjoint(residual)
    update2 = first - step_size * to_time(all_freq(grad2))
    threshold2 = threshold_of(update2)
    mine = lax.dynamic_slice_in_dim(update2, freq_pos * times_here, times_here, axis=0)
    mine = mine - jnp.clip(mine, -threshold2, threshold2)
    mine = mine.reshape(times_here, 2, quarter, 2, rows_v)
    own = mine[:, :, :, 0]
    other = swap(mine[:, :, :, 1])
    first_b = jnp.where(core == 0, own, other)
    second_b = jnp.where(core == 0, other, own)
    estimate = jnp.stack([first_b, second_b], axis=2).transpose(4, 0, 1, 2, 3)
    estimate = estimate.reshape(rows_v, times_here * sources)

    res_own = residual[:, :, :rows_u]
    res_other = swap(residual[:, :, rows_u:])
    lo = jnp.where(core == 0, res_own, res_other)
    hi = jnp.where(core == 0, res_other, res_own)
    residual_out = jnp.stack([lo, hi]).transpose(3, 2, 0, 1).reshape(1, rows_u, 2 * sources)
    return (estimate, residual_out)


def solution(mesh):
    placed = (
        P("freq", "tile", None),
        P(None, "freq", "tile", None),
        P(None, "freq", "tile", None),
        P("freq", None, None),
    )
    return jax.shard_map(
        local,
        mesh=mesh,
        in_specs=placed,
        out_specs=(P("tile", "freq"), P("freq", "tile", None)),
        check_vma=False,
    )
```

```python
import math

import jax
import jax.numpy as jnp
from jax import lax
from jax.experimental import pallas as pl
from jax.sharding import PartitionSpec as P

R = 64
TIMES = 16

step_size = 0.25
shrink_factor = 0.5
energy_floor = 1e-06
matmul_precision = lax.Precision.HIGH


def contract(form, left, right):
    return jnp.einsum(form, left, right, precision=matmul_precision)


def phases(freq_index, time_index, total_times):
    turn_count = (2 * freq_index[:, None] + 1) * time_index[None, :] % total_times
    angle_rad = turn_count.astype(jnp.float32) * (2.0 * math.pi / total_times)
    weight = 1.0 / math.sqrt(total_times)
    return (jnp.cos(angle_rad) * weight, jnp.sin(angle_rad) * weight)


def weight_kernel(own_ref, other_ref, out_ref):
    for jj in range(out_ref.shape[0]):
        lo, hi = jj * R, (jj + 1) * R
        re = jnp.concatenate([own_ref[0, :, lo:hi], other_ref[0, :, lo:hi]], axis=0)
        im = jnp.concatenate([own_ref[1, :, lo:hi], other_ref[1, :, lo:hi]], axis=0)
        rows = re.shape[0]
        out_ref[jj, :rows, :R] = re
        out_ref[jj, rows:, :R] = im
        out_ref[jj, :rows, R:] = -im
        out_ref[jj, rows:, R:] = re


def build_weights(own, other):
    rows, cols = own.shape[1], own.shape[2]
    tiles = cols // R
    per_step = min(tiles, 32)
    spec = pl.BlockSpec((2, rows, per_step * R), lambda p: (0, 0, p))
    return pl.pallas_call(
        weight_kernel,
        grid=(tiles // per_step,),
        in_specs=[spec, spec],
        out_specs=pl.BlockSpec((per_step, 4 * rows, 2 * R), lambda p: (p, 0, 0)),
        out_shape=jax.ShapeDtypeStruct((tiles, 4 * rows, 2 * R), own.dtype),
    )(own, other)

def half_weight_kernel(src_ref, out_ref):
    for jj in range(out_ref.shape[0]):
        lo, hi = jj * R, (jj + 1) * R
        re = src_ref[0, :, lo:hi]
        im = src_ref[1, :, lo:hi]
        rows = re.shape[0]
        out_ref[jj, :rows, :R] = re
        out_ref[jj, rows:, :R] = im
        out_ref[jj, :rows, R:] = -im
        out_ref[jj, rows:, R:] = re


def build_half_weights(src):
    rows, cols = src.shape[1], src.shape[2]
    tiles = cols // R
    per_step = min(tiles, 32)
    return pl.pallas_call(
        half_weight_kernel,
        grid=(tiles // per_step,),
        in_specs=[pl.BlockSpec((2, rows, per_step * R), lambda p: (0, 0, p))],
        out_specs=pl.BlockSpec((per_step, 2 * rows, 2 * R), lambda p: (p, 0, 0)),
        out_shape=jax.ShapeDtypeStruct((tiles, 2 * rows, 2 * R), src.dtype),
    )(src)


def local(observed, factor_u, factor_v, tile_ranks):
    tile_count = lax.axis_size("tile")
    freq_count = lax.axis_size("freq")
    position = lax.axis_index("tile")
    freq_pos = lax.axis_index("freq")
    core = position % 2
    column = position // 2
    rows_u = factor_u.shape[2]
    rows_v = factor_v.shape[2]
    row_tiles = factor_v.shape[3] // R
    col_tiles = factor_u.shape[3] // R
    sources = observed.shape[2] // 2
    half = sources // 2
    quarter = half // 2
    chips_per_row_tile = tile_count // row_tiles // 2
    times_here = TIMES // freq_count
    total_times = times_here * freq_count
    entries = rows_v * tile_count * total_times * sources
    chunk = (quarter, 2 * R)

    pair = [(k, k ^ 1) for k in range(tile_count)]

    def swap(x):
        return lax.ppermute(x, "tile", pair)

    u_own = factor_u[:, 0]
    v_own = factor_v[:, 0]
    obs_own = observed[0]
    u_other = swap(u_own)
    v_own, _ = lax.optimization_barrier((v_own, u_other))
    v_other = swap(v_own)
    obs_both = jnp.concatenate([obs_own, swap(obs_own)], axis=0)
    obs_split = obs_both.reshape(2 * rows_u, 2, 2, half)
    target = lax.dynamic_index_in_dim(obs_split, core, axis=2, keepdims=False).transpose(2, 1, 0)

    w_uo = build_half_weights(u_own)
    w_up = build_half_weights(u_other)
    w_v = build_weights(v_own, v_other)

    rank_column = lax.dynamic_index_in_dim(tile_ranks[0], column, axis=1, keepdims=False)
    rank_mask = (jnp.arange(R, dtype=jnp.int32)[None, :] < rank_column[:, None]).astype(jnp.float32)
    rank_mask = jnp.concatenate([rank_mask, rank_mask], axis=1)

    all_freqs = jnp.arange(freq_count, dtype=jnp.int32)
    all_times = jnp.arange(total_times, dtype=jnp.int32)
    cos_tab, sin_tab = phases(all_freqs, all_times, total_times)

    def adjoint(resid):
        lhs_o = resid[:, :, :rows_u].reshape(half, 2 * rows_u)
        lhs_p = resid[:, :, rows_u:].reshape(half, 2 * rows_u)
        e = contract("vq,jqo->jvo", lhs_o, w_uo) + contract("vq,jqo->jvo", lhs_p, w_up)
        outgoing = e.reshape((tile_count,) + chunk)
        incoming = lax.all_to_all(outgoing, "tile", 0, 0, tiled=True)
        gathered = incoming.reshape((row_tiles, chips_per_row_tile, 2) + chunk).sum(axis=1)
        gathered = gathered.reshape(row_tiles, half, 2 * R) * rank_mask[:, None, :]
        blocks = contract("ivo,iqo->ivq", gathered, w_v).sum(axis=0)
        return blocks.reshape(half, 2, 2 * rows_v)

    def all_freq(spectrum):
        outgoing = jnp.broadcast_to(spectrum[None], (freq_count,) + spectrum.shape)
        return lax.all_to_all(outgoing, "freq", 0, 0, tiled=True)

    def to_time(spectra):
        total = 0.0
        for f in range(freq_count):
            total = total + (
                cos_tab[f][:, None, None] * spectra[f, :, 0][None]
                - sin_tab[f][:, None, None] * spectra[f, :, 1][None]
            )
        return total

    def threshold_of(update):
        energy = jnp.sum(update * update)
        outgoing = jnp.broadcast_to(energy, (tile_count, 1))
        total = jnp.sum(lax.all_to_all(outgoing, "tile", 0, 0, tiled=True))
        return shrink_factor * jnp.sqrt(total / entries + energy_floor)

    grad1 = adjoint(target)
    update1 = step_size * to_time(all_freq(grad1))
    threshold1 = threshold_of(update1)
    first = update1 - jnp.clip(update1, -threshold1, threshold1)

    cos_q = lax.dynamic_index_in_dim(cos_tab, freq_pos, axis=0, keepdims=False)
    sin_q = lax.dynamic_index_in_dim(sin_tab, freq_pos, axis=0, keepdims=False)
    x_re = jnp.sum(cos_q[:, None, None] * first, axis=0)
    x_im = -jnp.sum(sin_q[:, None, None] * first, axis=0)
    lhs = jnp.stack([x_re, x_im], axis=1).reshape(half, 2 * 2 * rows_v)
    coeffs = contract("vq,iqo->ivo", lhs, w_v) * rank_mask[:, None, :]
    outgoing = jnp.broadcast_to(
        coeffs.reshape((row_tiles, 1, 2) + chunk),
        (row_tiles, chips_per_row_tile, 2) + chunk,
    ).reshape((tile_count,) + chunk)
    incoming = lax.all_to_all(outgoing, "tile", 0, 0, tiled=True)
    summed = incoming.reshape(col_tiles, half, 2 * R)
    y_o = contract("jvo,jqo->jvq", summed, w_uo).sum(axis=0).reshape(half, 2, rows_u)
    y_p = contract("jvo,jqo->jvq", summed, w_up).sum(axis=0).reshape(half, 2, rows_u)
    residual = jnp.concatenate([y_o, y_p], axis=2) - target

    grad2 = adjoint(residual)
    update2 = first - step_size * to_time(all_freq(grad2))
    threshold2 = threshold_of(update2)
    mine = lax.dynamic_slice_in_dim(update2, freq_pos * times_here, times_here, axis=0)
    mine = mine - jnp.clip(mine, -threshold2, threshold2)
    mine = mine.reshape(times_here, 2, quarter, 2, rows_v)
    own = mine[:, :, :, 0]
    other = swap(mine[:, :, :, 1])
    first_b = jnp.where(core == 0, own, other)
    second_b = jnp.where(core == 0, other, own)
    estimate = jnp.stack([first_b, second_b], axis=2).transpose(4, 0, 1, 2, 3)
    estimate = estimate.reshape(rows_v, times_here * sources)

    res_own = residual[:, :, :rows_u]
    res_other = swap(residual[:, :, rows_u:])
    lo = jnp.where(core == 0, res_own, res_other)
    hi = jnp.where(core == 0, res_other, res_own)
    residual_out = jnp.stack([lo, hi]).transpose(3, 2, 0, 1).reshape(1, rows_u, 2 * sources)
    return (estimate, residual_out)


def solution(mesh):
    placed = (
        P("freq", "tile", None),
        P(None, "freq", "tile", None),
        P(None, "freq", "tile", None),
        P("freq", None, None),
    )
    return jax.shard_map(
        local,
        mesh=mesh,
        in_specs=placed,
        out_specs=(P("tile", "freq"), P("freq", "tile", None)),
        check_vma=False,
    )
```
